512 devices in a mesh: seq: 64 (over x, y, core), tp: 8 (over z).
Axes of the slice: x: 4, y: 8, z: 8, core: 2. Of those that a mesh axis runs over, the one named last changes fastest.
Arguments:
- x_proj: bfloat16 [32768, 8192], P('seq', 'tp'), may hold values from -27 to 27
- bc_proj: bfloat16 [32768, 2, 1024], P('seq', None, 'tp'), may hold values from -6 to 6
- z_proj: bfloat16 [32768, 8192], P('seq', 'tp'), may hold values from -6 to 6
- dt_raw: float32 [32768, 128], P('seq', 'tp'), may hold values from -2.5 to 63
- conv_x: bfloat16 [4, 8192], P(None, 'tp'), may hold values from -3 to 3
- conv_bc: bfloat16 [4, 2, 1024], P(None, None, 'tp'), may hold values from -3 to 3
- bias_x: float32 [8192], P('tp'), may hold values from -0.5 to 0.5
- bias_bc: float32 [2, 1024], P(None, 'tp'), may hold values from -0.5 to 0.5
- dt_bias: float32 [128], P('tp'), may hold values from -4.5 to -3
- a_log: float32 [128], P('tp'), may hold values from -5.5 to 0.5
- d_skip: float32 [128], P('tp'), may hold values from 0.15 to 5
- norm_gain: float32 [8192], P('tp'), may hold values from 0.1 to 1.9
- seg_ids: int32 [32768], P('seq'), may hold values from 0 to 15, never falling along the last dimension, each value on 1 to 8192 neighbouring positions
Outputs:
- normed: bfloat16 [32768, 8192], P('seq', 'tp')
The draws below stay inside these ranges and needn't reach their ends.
Inputs may be any that keep to these rules, and one draw needn't show every extreme that they name: `seg_ids`: each prompt's tokens are contiguous; ids start at 0 and never fall, each id from 0 to 15 has one token or more, at most 8192 tokens, and one prompt has exactly 8192.
All inputs are finite; a program needn't handle non-finite values.
Results may differ from the reference program's by a relative error of at most 0.0036.
Values may be sent and summed in bfloat16 or wider, within the bound.
No kernel may reach another device: no remote copies, remote signals or barrier semaphores. Data moves between devices by JAX's collectives and lax.ppermute only.
A program may use at most 128 MiB of HBM per device.

```python
import math
import jax
import jax.numpy as jnp
import numpy as np
from jax import lax

HEADS = 128
HEAD_DIM = 64
GROUPS = 8
STATE = 128
CONV_K = 4
STRETCH = 256
TOK_DEV = 512
REQS = 16
INNER = 8192
PACKED_TOKENS = 32768
MOST = 8192


def draw_x_proj(key, part):
    row_key, col_key, value_key = jax.random.split(key, 3)
    row_scale = jnp.exp(jax.random.uniform(row_key, (PACKED_TOKENS, 1)) * math.log(10.0)) * 0.3
    col_scale = jnp.exp(jax.random.uniform(col_key, (1, INNER)) * math.log(10.0)) * 0.3
    values = jnp.clip(jax.random.normal(value_key, (PACKED_TOKENS, INNER)), -3.0, 3.0) * row_scale * col_scale
    return values.astype(jnp.bfloat16)


def draw_dt_raw(key, part):
    jitter_random_key, block_random_key, spike_random_key = jax.random.split(key, 3)
    random_jitter = jnp.clip(jax.random.normal(jitter_random_key, (PACKED_TOKENS, HEADS)) * 0.5, -1.5, 1.5)
    block_shift = jax.random.uniform(block_random_key, (PACKED_TOKENS // TOK_DEV, HEADS), minval=-0.7, maxval=0.7)
    moved_values = jnp.repeat(block_shift, TOK_DEV, axis=0)
    chosen_positions = jax.random.randint(spike_random_key, (8,), 0, PACKED_TOKENS)
    spike_values = jnp.any(jnp.arange(PACKED_TOKENS)[:, None] == chosen_positions[None, :], axis=1).astype(jnp.float32)
    return (random_jitter + moved_values + 60.0 * spike_values[:, None]).astype(jnp.float32)


def draw_a_log(key, part):
    kind_key, slow_key, fast_key = jax.random.split(key, 3)
    slow = jax.random.uniform(slow_key, (HEADS,), minval=-5.5, maxval=-4.8)
    chosen = jax.random.bernoulli(kind_key, 0.5, (HEADS,))
    fast = jax.random.uniform(fast_key, (HEADS,), minval=-2.0, maxval=0.5)
    return jnp.where(chosen, slow, fast).astype(jnp.float32)


def draw_d_skip(key, part):
    order = jnp.arange(HEADS, dtype=jnp.float32) / HEADS
    base = jnp.exp(math.log(0.3) + math.log(10.0) * order)
    factor = jax.random.uniform(key, (HEADS,), minval=0.8, maxval=1.25)
    return (base * factor).astype(jnp.float32)


def steps_of(own_key, extent, shards, least, top_value):
    def one(position, shards_of):
        steps = jax.random.uniform(jax.random.fold_in(jax.random.fold_in(own_key, 6), position), (shards_of,), jnp.float32, least / len(shards), top_value / len(shards))
        return jnp.repeat(jnp.exp(steps), extent[position] // shards_of).reshape((-1,) + (1,) * (len(extent) - position - 1))

    gain = one(*shards[0])
    for cut in shards[1:]:
        gain = gain * one(*cut)
    return gain


def length_profile(amount, total, most, lean):
    portions = [(1 << 20) // math.isqrt(rank ** lean) + 1 for rank in range(2, amount + 1)]
    surplus, given = total - most - (amount - 1), [1] * (amount - 1)
    while surplus > 0:
        candidates = [i for i in range(amount - 1) if given[i] < most]
        mass, remaining = sum([portions[i] for i in candidates]), surplus
        for i in candidates:
            addition = min(most - given[i], max(1, remaining * portions[i] // mass), surplus)
            given[i] = given[i] + addition
            surplus = surplus - addition
    return np.array([most] + given)


def uneven_parts(stream_key, count, total, limit, slope):
    if count == 2:
        one = jax.random.randint(stream_key, (), max(1, total - limit), min(limit, total - 1) + 1)
        return jnp.stack([one, total - one])
    lengths = jnp.asarray(length_profile(count, total, limit, slope), jnp.int32)
    twos = (count - 1) // 2
    donor, receiver = lengths[1:1 + 2 * twos:2], lengths[2:2 + 2 * twos:2]
    room = jnp.minimum(donor - 1, limit - receiver)
    passed = jax.random.randint(jax.random.fold_in(stream_key, 1), (twos,), 0, 1 << 20) % (room + 1)
    lengths = lengths.at[1:1 + 2 * twos:2].set(donor - passed).at[2:2 + 2 * twos:2].set(receiver + passed)
    return lengths[jax.random.permutation(jax.random.fold_in(stream_key, 2), count)]


def gaussian(own_key, dims, deviation, reach, cuts=(), kind=jnp.bfloat16):
    drawn = jax.random.normal(own_key, dims, jnp.float32) * deviation
    if len(cuts) > 0:
        drawn = steps_of(own_key, dims, cuts, -0.22, 0.18) * drawn
    return jnp.clip(drawn, min=-reach, max=reach).astype(kind)


def setup_inputs(seed: int = 0) -> dict:
    key_of = jax.random.split(jax.random.key(seed), 14)
    return {
        "x_proj": draw_x_proj(jax.random.fold_in(key_of[13], 71), 0),
        "bc_proj": gaussian(key_of[1], (PACKED_TOKENS, 2, GROUPS * STATE), 1.0, 6.0, ((0, 64), (2, 8))),
        "z_proj": gaussian(key_of[2], (PACKED_TOKENS, INNER), 1.0, 6.0, ((0, 64), (1, 8))),
        "dt_raw": draw_dt_raw(jax.random.fold_in(key_of[13], 71), 0),
        "conv_x": gaussian(key_of[4], (CONV_K, INNER), CONV_K ** -0.5, 3.0, ((1, 8),)),
        "conv_bc": gaussian(key_of[5], (CONV_K, 2, GROUPS * STATE), CONV_K ** -0.5, 3.0, ((2, 8),)),
        "bias_x": jnp.clip(jax.random.uniform(key_of[6], (INNER,), jnp.float32, -0.5, 0.5) * steps_of(key_of[6], (INNER,), ((0, 8),), -0.4, 0.0), -0.5, 0.5),
        "bias_bc": jnp.clip(jax.random.uniform(key_of[7], (2, GROUPS * STATE), jnp.float32, -0.5, 0.5) * steps_of(key_of[7], (2, GROUPS * STATE), ((1, 8),), -0.4, 0.0), -0.5, 0.5),
        "dt_bias": jnp.clip(-4.5 + 1.5 * jax.random.uniform(key_of[8], (HEADS,), jnp.float32) ** steps_of(key_of[8], (HEADS,), ((0, 8),), -0.2, 0.2), -4.5, -3.0),
        "a_log": draw_a_log(jax.random.fold_in(key_of[13], 71), 0),
        "d_skip": draw_d_skip(jax.random.fold_in(key_of[13], 71), 0),
        "norm_gain": jnp.clip(1.0 + 0.18 * jax.random.normal(key_of[11], (INNER,), jnp.float32), 0.1, 1.9),
        "seg_ids": jnp.searchsorted(jnp.cumsum(uneven_parts(key_of[12], REQS, PACKED_TOKENS, MOST, 2)), jnp.arange(PACKED_TOKENS), side="right").astype(jnp.int32),
    }


def causal_conv(window, window_ids, weight, bias, rows):
    taps = weight.shape[0]
    own_ids = window_ids[taps - 1:]
    extra = (1,) * (window.ndim - 1)
    result = jnp.broadcast_to(bias.astype(jnp.float32), (rows,) + bias.shape)
    for offset in range(taps):
        piece = window[offset:offset + rows].astype(jnp.float32)
        same = (window_ids[offset:offset + rows] == own_ids).reshape((rows,) + extra)
        result = result + jnp.where(same, piece * weight[offset].astype(jnp.float32), 0.0)
    return jax.nn.silu(result).astype(jnp.bfloat16)

def reference(x_proj, bc_proj, z_proj, dt_raw, conv_x, conv_bc, bias_x, bias_bc, dt_bias, a_log, d_skip, norm_gain, seg_ids):
    heads_group = HEADS // GROUPS
    margin = CONV_K - 1
    token_ids = seg_ids.astype(jnp.float32)
    x_pad = jnp.concatenate([jnp.zeros((margin, INNER), jnp.bfloat16), x_proj])
    bc_pad = jnp.concatenate([jnp.zeros((margin, 2, GROUPS * STATE), jnp.bfloat16), bc_proj])
    id_pad = jnp.concatenate([jnp.zeros((margin,), jnp.float32), token_ids])
    rate = -jnp.exp(a_log)
    lower = jnp.tril(jnp.ones((STRETCH, STRETCH), dtype=bool))
    skip = d_skip.reshape(GROUPS, heads_group)[..., None]

    def advance(state, index):
        begin = (index * STRETCH).astype(jnp.int32)
        x_window = lax.dynamic_slice_in_dim(x_pad, begin, STRETCH + margin, 0)
        bc_window = lax.dynamic_slice_in_dim(bc_pad, begin, STRETCH + margin, 0)
        id_window = lax.dynamic_slice_in_dim(id_pad, begin, STRETCH + margin, 0)
        own = id_window[margin:]
        before = id_window[margin - 1]
        x_conv = causal_conv(x_window, id_window, conv_x, bias_x, STRETCH)
        bc_conv = causal_conv(bc_window, id_window, conv_bc, bias_bc, STRETCH)
        step_size = jax.nn.softplus(lax.dynamic_slice_in_dim(dt_raw, begin, STRETCH, 0) + dt_bias)
        cumul = jnp.cumsum(step_size * rate, axis=0)
        cum_heads = cumul.T.reshape(GROUPS, heads_group, STRETCH)
        step_heads = step_size.T.reshape(GROUPS, heads_group, STRETCH)
        b_in = bc_conv[:, 0].reshape(STRETCH, GROUPS, STATE).astype(jnp.float32)
        c_out = bc_conv[:, 1].reshape(STRETCH, GROUPS, STATE).astype(jnp.float32)
        same = (own[:, None] == own[None, :]) & lower
        scores = jnp.einsum('qgn,sgn->gqs', c_out, b_in)
        spread = cum_heads[..., :, None] - cum_heads[..., None, :]
        decay = jnp.where(same, jnp.exp(jnp.where(same, spread, 0.0)), 0.0)
        mixing = (scores[:, None] * decay * step_heads[:, :, None, :]).astype(jnp.bfloat16)
        x_heads = x_conv.reshape(STRETCH, GROUPS, heads_group, HEAD_DIM).astype(jnp.float32)
        y_intra = jnp.einsum('ghqs,sghp->qghp', mixing.astype(jnp.float32), x_heads)
        tail_same = (own == own[-1]).astype(jnp.float32)
        weights = jnp.exp(cum_heads[..., -1:] - cum_heads) * step_heads * tail_same
        b_weighted = (jnp.transpose(b_in, (1, 0, 2))[:, None] * weights[..., None]).astype(jnp.bfloat16)
        increment = jnp.einsum('ghsn,sghp->ghpn', b_weighted.astype(jnp.float32), x_heads)
        carry_gain = jnp.exp(cum_heads[..., -1]) * (own[-1] == before).astype(jnp.float32)
        link = jnp.exp(cum_heads) * (own == before).astype(jnp.float32)
        y_inter = jnp.einsum('qgn,ghpn->qghp', c_out, state, precision=lax.Precision.HIGHEST) * jnp.transpose(link, (2, 0, 1))[..., None]
        new_state = carry_gain[..., None, None] * state + increment
        mixed = y_intra + y_inter + skip * x_heads
        z_block = lax.dynamic_slice_in_dim(z_proj, begin, STRETCH, 0).astype(jnp.float32)
        gated = mixed.reshape(STRETCH, INNER) * jax.nn.silu(z_block)
        scale = lax.rsqrt(lax.optimization_barrier(jnp.sum(gated * gated, axis=-1)) / INNER + 1e-05)
        return (new_state, (gated * scale[:, None] * norm_gain).astype(jnp.bfloat16))
    start_state = jnp.zeros((GROUPS, heads_group, HEAD_DIM, STATE), jnp.float32)
    _, outputs = lax.scan(advance, start_state, jnp.arange(PACKED_TOKENS // STRETCH, dtype=jnp.int32))
    return outputs.reshape(PACKED_TOKENS, INNER)
```

```python
import jax
import jax.numpy as jnp
from jax import lax
from jax.sharding import PartitionSpec as P

STATE = 128
STRETCH = 256


def from_behind(block, axis, distance):
    devices = range(lax.axis_size(axis))
    route = [(i - distance, i) for i in devices if i - distance in devices]
    return lax.ppermute(block, axis, route)


def shifted(block, axis, pairs):
    return lax.ppermute(block, axis, pairs)


def fold(earlier, later):
    gain_e, state_e = earlier
    gain_l, state_l = later
    return (gain_e * gain_l, gain_l[..., None, None] * state_e + state_l)


def entering_state(gain, state, axis):
    count = lax.axis_size(axis)
    chips = count // 2
    own = (gain, state)
    pair = shifted(own, axis, [(2 * c, 2 * c + 1) for c in range(chips)])
    chip_total = fold(pair, own)
    for reach in (1, 2, 4):
        route = [(2 * c + 1, 2 * (c + reach) + 1) for c in range(chips - reach)]
        chip_total = fold(shifted(chip_total, axis, route), chip_total)
    behind = shifted(chip_total[1], axis, [(2 * c - 1, 2 * c) for c in range(1, chips)])
    passed = gain[..., None, None] * behind + state
    ahead = shifted(passed, axis, [(2 * c, 2 * c + 1) for c in range(chips)])
    mine = lax.axis_index(axis)
    return jnp.where(mine % 2 == 0, behind, ahead)


def causal_conv(window, window_ids, weight, bias, rows):
    taps = weight.shape[0]
    own_ids = window_ids[taps - 1 :]
    extra = (1,) * (window.ndim - 1)
    result = jnp.broadcast_to(bias, (rows,) + bias.shape)
    for offset in range(taps):
        piece = window[offset : offset + rows].astype(jnp.float32)
        same = (window_ids[offset : offset + rows] == own_ids).reshape((rows,) + extra)
        result = result + jnp.where(same, piece * weight[offset].astype(jnp.float32), 0.0)
    return jax.nn.silu(result).astype(jnp.bfloat16)


def on_device(
    x_proj,
    bc_proj,
    z_proj,
    dt_raw,
    conv_x,
    conv_bc,
    bias_x,
    bias_bc,
    dt_bias,
    a_log,
    d_skip,
    norm_gain,
    seg_ids,
):
    tok_rows, inner_local = x_proj.shape
    heads_local = dt_raw.shape[1]
    state_size = STATE
    groups_local = bc_proj.shape[2] // state_size
    heads_group = heads_local // groups_local
    head_size = inner_local // heads_local
    block = STRETCH
    blocks = tok_rows // block
    margin = conv_x.shape[0] - 1
    tails = (
        x_proj[tok_rows - margin :],
        bc_proj[tok_rows - margin :],
        seg_ids[tok_rows - margin :].astype(jnp.bfloat16),
    )
    rim_x, rim_bc, rim_ids = from_behind((tails[0], tails[1], tails[2]), "seq", 1)
    own_ids = seg_ids.astype(jnp.float32)
    window_ids = jnp.concatenate([rim_ids.astype(jnp.float32), own_ids])
    x_conv = causal_conv(jnp.concatenate([rim_x, x_proj]), window_ids, conv_x, bias_x, tok_rows)
    bc_conv = causal_conv(
        jnp.concatenate([rim_bc, bc_proj]), window_ids, conv_bc, bias_bc, tok_rows
    )
    step_size = jax.nn.softplus(dt_raw + dt_bias)
    log_decay = step_size * -jnp.exp(a_log)
    cumul = jnp.cumsum(log_decay.reshape(blocks, block, heads_local), axis=1)
    cum_heads = cumul.reshape(blocks, block, groups_local, heads_group).transpose(0, 2, 3, 1)
    step_heads = step_size.reshape(blocks, block, groups_local, heads_group).transpose(0, 2, 3, 1)
    block_ids = own_ids.reshape(blocks, block)
    before_ids = window_ids[margin - 1 : margin - 1 + tok_rows : block]
    b_in = bc_conv[:, 0].reshape(blocks, block, groups_local, state_size)
    c_out = bc_conv[:, 1].reshape(blocks, block, groups_local, state_size)
    lower = jnp.tril(jnp.ones((block, block), dtype=bool))
    same = (block_ids[:, :, None] == block_ids[:, None, :]) & lower
    scores = jnp.einsum("cqgn,csgn->cgqs", c_out, b_in, preferred_element_type=jnp.float32)
    same_heads = same[:, None, None]
    spread = cum_heads[..., :, None] - cum_heads[..., None, :]
    decay = jnp.where(same_heads, jnp.exp(jnp.where(same_heads, spread, 0.0)), 0.0)
    mixing = (scores[:, :, None] * decay * step_heads[..., None, :]).astype(jnp.bfloat16)
    x_heads = x_conv.reshape(blocks, block, groups_local, heads_group, head_size)
    y_intra = jnp.einsum("cghqs,csghp->cqghp", mixing, x_heads, preferred_element_type=jnp.float32)
    tail_same = (block_ids == block_ids[:, -1:]).astype(jnp.float32)[:, None, None, :]
    weights = jnp.exp(cum_heads[..., -1:] - cum_heads) * step_heads * tail_same
    b_weighted = (
        b_in.transpose(0, 2, 1, 3)[:, :, None].astype(jnp.float32) * weights[..., None]
    ).astype(jnp.bfloat16)
    increment = jnp.einsum(
        "cghsn,csghp->cghpn", b_weighted, x_heads, preferred_element_type=jnp.float32
    )
    carry_gain = (
        jnp.exp(cum_heads[..., -1])
        * (block_ids[:, -1] == before_ids).astype(jnp.float32)[:, None, None]
    )
    link = (
        jnp.exp(cum_heads)
        * (block_ids == before_ids[:, None]).astype(jnp.float32)[:, None, None, :]
    )
    c_float = c_out.astype(jnp.float32)

    def recur(start_state):
        stacked = []
        current = start_state
        for index in range(blocks):
            stacked.append(current)
            current = carry_gain[index][..., None, None] * current + increment[index]
        return (jnp.stack(stacked), current)

    empty = jnp.zeros((groups_local, heads_group, head_size, state_size), jnp.float32)
    zero_states, summary = recur(empty)
    device_gain = carry_gain[0] * carry_gain[1]
    entering = entering_state(device_gain, summary, "seq")
    states, _ = recur(entering)
    product = jnp.einsum("cqgn,cghpn->cqghp", c_float, states, precision=lax.Precision.HIGHEST)
    y_inter = product * link.transpose(0, 3, 1, 2)[..., None]
    skip = d_skip.reshape(groups_local, heads_group)[..., None]
    mixed = y_intra + y_inter + skip * x_heads.astype(jnp.float32)
    gated = mixed.reshape(tok_rows, inner_local) * jax.nn.silu(z_proj.astype(jnp.float32))
    squares = lax.psum(jnp.sum(gated * gated, axis=-1), "tp")
    scale = lax.rsqrt(squares / (inner_local * lax.axis_size("tp")) + 1e-05)
    return (gated * scale[:, None] * norm_gain).astype(jnp.bfloat16)


def solution(mesh):
    in_specs = (
        P("seq", "tp"),
        P("seq", None, "tp"),
        P("seq", "tp"),
        P("seq", "tp"),
        P(None, "tp"),
        P(None, None, "tp"),
        P("tp"),
        P(None, "tp"),
        P("tp"),
        P("tp"),
        P("tp"),
        P("tp"),
        P("seq"),
    )
    out_specs = P("seq", "tp")
    return jax.shard_map(
        on_device, mesh=mesh, in_specs=in_specs, out_specs=out_specs, check_vma=False
    )
```

```python
import jax
import jax.numpy as jnp
from jax import lax
from jax.sharding import PartitionSpec as P

STATE = 128
STRETCH = 256


def from_behind(block, axis, distance):
    devices = range(lax.axis_size(axis))
    route = [(i - distance, i) for i in devices if i - distance in devices]
    return lax.ppermute(block, axis, route)


def shifted(block, axis, pairs):
    return lax.ppermute(block, axis, pairs)


def fold(earlier, later):
    gain_e, state_e = earlier
    gain_l, state_l = later
    return (gain_e * gain_l, gain_l[..., None, None] * state_e + state_l)


def pack(gain, state):
    lanes = state.shape[-1]
    flat = state.reshape(-1, lanes)
    row = jnp.zeros((8, lanes), state.dtype).at[0, : gain.size].set(gain.reshape(-1))
    return jnp.concatenate([flat, row])


def unpack(packed, gain_shape, state_shape):
    rows = packed.shape[0] - 8
    count = 1
    for size in gain_shape:
        count *= size
    return (packed[rows, :count].reshape(gain_shape), packed[:rows].reshape(state_shape))


def entering_state(gain, state, axis):
    count = lax.axis_size(axis)
    chips = count // 2
    shapes = (gain.shape, state.shape)
    own = (gain, state)
    pair = unpack(shifted(pack(*own), axis, [(2 * c, 2 * c + 1) for c in range(chips)]), *shapes)
    chip_total = fold(pair, own)
    for reach in (1, 2, 4):
        route = [(2 * c + 1, 2 * (c + reach) + 1) for c in range(chips - reach)]
        got = unpack(shifted(pack(*chip_total), axis, route), *shapes)
        chip_total = fold(got, chip_total)
    to_even = shifted(chip_total[1], axis, [(2 * c - 1, 2 * c) for c in range(1, chips)])
    to_odd = shifted(chip_total[1], axis, [(2 * c - 1, 2 * c + 1) for c in range(1, chips)])
    odd_entering = pair[0][..., None, None] * to_odd + pair[1]
    mine = lax.axis_index(axis)
    return jnp.where(mine % 2 == 0, to_even, odd_entering)


def summed_over(value, axis):
    count = lax.axis_size(axis)
    if count & (count - 1):
        return lax.psum(value, axis)
    reach = 1
    while reach < count:
        value = value + lax.ppermute(value, axis, [(i, i ^ reach) for i in range(count)])
        reach *= 2
    return value


def causal_conv(window, window_ids, weight, bias, rows):
    taps = weight.shape[0]
    own_ids = window_ids[taps - 1 :]
    extra = (1,) * (window.ndim - 1)
    result = jnp.broadcast_to(bias, (rows,) + bias.shape)
    for offset in range(taps):
        piece = window[offset : offset + rows].astype(jnp.float32)
        same = (window_ids[offset : offset + rows] == own_ids).reshape((rows,) + extra)
        result = result + jnp.where(same, piece * weight[offset].astype(jnp.float32), 0.0)
    return jax.nn.silu(result).astype(jnp.bfloat16)


def on_device(
    x_proj,
    bc_proj,
    z_proj,
    dt_raw,
    conv_x,
    conv_bc,
    bias_x,
    bias_bc,
    dt_bias,
    a_log,
    d_skip,
    norm_gain,
    seg_ids,
):
    tok_rows, inner_local = x_proj.shape
    heads_local = dt_raw.shape[1]
    state_size = STATE
    groups_local = bc_proj.shape[2] // state_size
    heads_group = heads_local // groups_local
    head_size = inner_local // heads_local
    block = STRETCH
    blocks = tok_rows // block
    margin = conv_x.shape[0] - 1
    tails = (
        x_proj[tok_rows - margin :],
        bc_proj[tok_rows - margin :],
        seg_ids[tok_rows - margin :].astype(jnp.bfloat16),
    )
    rim_x, rim_bc, rim_ids = from_behind((tails[0], tails[1], tails[2]), "seq", 1)
    own_ids = seg_ids.astype(jnp.float32)
    window_ids = jnp.concatenate([rim_ids.astype(jnp.float32), own_ids])
    x_conv = causal_conv(jnp.concatenate([rim_x, x_proj]), window_ids, conv_x, bias_x, tok_rows)
    bc_conv = causal_conv(
        jnp.concatenate([rim_bc, bc_proj]), window_ids, conv_bc, bias_bc, tok_rows
    )
    step_size = jax.nn.softplus(dt_raw + dt_bias)
    log_decay = step_size * -jnp.exp(a_log)
    cumul = jnp.cumsum(log_decay.reshape(blocks, block, heads_local), axis=1)
    cum_heads = cumul.reshape(blocks, block, groups_local, heads_group).transpose(0, 2, 3, 1)
    step_heads = step_size.reshape(blocks, block, groups_local, heads_group).transpose(0, 2, 3, 1)
    block_ids = own_ids.reshape(blocks, block)
    before_ids = window_ids[margin - 1 : margin - 1 + tok_rows : block]
    b_in = bc_conv[:, 0].reshape(blocks, block, groups_local, state_size)
    c_out = bc_conv[:, 1].reshape(blocks, block, groups_local, state_size)
    lower = jnp.tril(jnp.ones((block, block), dtype=bool))
    same = (block_ids[:, :, None] == block_ids[:, None, :]) & lower
    scores = jnp.einsum("cqgn,csgn->cgqs", c_out, b_in, preferred_element_type=jnp.float32)
    same_heads = same[:, None, None]
    spread = cum_heads[..., :, None] - cum_heads[..., None, :]
    decay = jnp.where(same_heads, jnp.exp(jnp.where(same_heads, spread, 0.0)), 0.0)
    mixing = (scores[:, :, None] * decay * step_heads[..., None, :]).astype(jnp.bfloat16)
    x_heads = x_conv.reshape(blocks, block, groups_local, heads_group, head_size)
    y_intra = jnp.einsum("cghqs,csghp->cqghp", mixing, x_heads, preferred_element_type=jnp.float32)
    tail_same = (block_ids == block_ids[:, -1:]).astype(jnp.float32)[:, None, None, :]
    weights = jnp.exp(cum_heads[..., -1:] - cum_heads) * step_heads * tail_same
    b_weighted = (
        b_in.transpose(0, 2, 1, 3)[:, :, None].astype(jnp.float32) * weights[..., None]
    ).astype(jnp.bfloat16)
    increment = jnp.einsum(
        "cghsn,csghp->cghpn", b_weighted, x_heads, preferred_element_type=jnp.float32
    )
    carry_gain = (
        jnp.exp(cum_heads[..., -1])
        * (block_ids[:, -1] == before_ids).astype(jnp.float32)[:, None, None]
    )
    link = (
        jnp.exp(cum_heads)
        * (block_ids == before_ids[:, None]).astype(jnp.float32)[:, None, None, :]
    )
    c_float = c_out.astype(jnp.float32)

    def recur(start_state):
        stacked = []
        current = start_state
        for index in range(blocks):
            stacked.append(current)
            current = carry_gain[index][..., None, None] * current + increment[index]
        return (jnp.stack(stacked), current)

    empty = jnp.zeros((groups_local, heads_group, head_size, state_size), jnp.float32)
    zero_states, summary = recur(empty)
    device_gain = carry_gain[0] * carry_gain[1]
    entering = entering_state(device_gain, summary, "seq")
    states, _ = recur(entering)
    product = jnp.einsum("cqgn,cghpn->cqghp", c_float, states, precision=lax.Precision.HIGHEST)
    y_inter = product * link.transpose(0, 3, 1, 2)[..., None]
    skip = d_skip.reshape(groups_local, heads_group)[..., None]
    mixed = y_intra + y_inter + skip * x_heads.astype(jnp.float32)
    gated = mixed.reshape(tok_rows, inner_local) * jax.nn.silu(z_proj.astype(jnp.float32))
    squares = summed_over(jnp.sum(gated * gated, axis=-1), "tp")
    scale = lax.rsqrt(squares / (inner_local * lax.axis_size("tp")) + 1e-05)
    return (gated * scale[:, None] * norm_gain).astype(jnp.bfloat16)


def solution(mesh):
    in_specs = (
        P("seq", "tp"),
        P("seq", None, "tp"),
        P("seq", "tp"),
        P("seq", "tp"),
        P(None, "tp"),
        P(None, None, "tp"),
        P("tp"),
        P(None, "tp"),
        P("tp"),
        P("tp"),
        P("tp"),
        P("tp"),
        P("seq"),
    )
    out_specs = P("seq", "tp")
    return jax.shard_map(
        on_device, mesh=mesh, in_specs=in_specs, out_specs=out_specs, check_vma=False
    )
```

```python
import jax
import jax.numpy as jnp
from jax import lax
from jax.sharding import PartitionSpec as P

STATE = 128
STRETCH = 256


def from_behind(block, axis, distance):
    devices = range(lax.axis_size(axis))
    route = [(i - distance, i) for i in devices if i - distance in devices]
    return lax.ppermute(block, axis, route)


def shifted(block, axis, pairs):
    return lax.ppermute(block, axis, pairs)


def fold(earlier, later):
    gain_e, state_e = earlier
    gain_l, state_l = later
    return (gain_e * gain_l, gain_l[..., None, None] * state_e + state_l)


def pack(gain, state):
    lanes = state.shape[-1]
    flat = state.reshape(-1, lanes)
    row = jnp.zeros((8, lanes), state.dtype).at[0, : gain.size].set(gain.reshape(-1))
    return jnp.concatenate([flat, row])


def unpack(packed, gain_shape, state_shape):
    rows = packed.shape[0] - 8
    count = 1
    for size in gain_shape:
        count *= size
    return (packed[rows, :count].reshape(gain_shape), packed[:rows].reshape(state_shape))


def entering_state(gain, state, axis, ride):
    count = lax.axis_size(axis)
    chips = count // 2
    shapes = (gain.shape, state.shape)
    own = (gain, state)
    pair = unpack(shifted(pack(*own), axis, [(2 * c, 2 * c + 1) for c in range(chips)]), *shapes)
    chip_total = fold(pair, own)
    for reach in (1, 2, 4):
        route = [(2 * c + 1, 2 * (c + reach) + 1) for c in range(chips - reach)]
        got = unpack(shifted(pack(*chip_total), axis, route), *shapes)
        if reach == 4:
            got, ride = lax.optimization_barrier((got, ride))
        chip_total = fold(got, chip_total)
    to_even = shifted(chip_total[1], axis, [(2 * c - 1, 2 * c) for c in range(1, chips)])
    to_odd = shifted(chip_total[1], axis, [(2 * c - 1, 2 * c + 1) for c in range(1, chips)])
    odd_entering = pair[0][..., None, None] * to_odd + pair[1]
    mine = lax.axis_index(axis)
    return jnp.where(mine % 2 == 0, to_even, odd_entering), ride


def summed_over(value, axis):
    count = lax.axis_size(axis)
    if count & (count - 1):
        return lax.psum(value, axis)
    reach = 1
    while reach < count:
        value = value + lax.ppermute(value, axis, [(i, i ^ reach) for i in range(count)])
        reach *= 2
    return value


def causal_conv(window, window_ids, weight, bias, rows):
    taps = weight.shape[0]
    own_ids = window_ids[taps - 1 :]
    extra = (1,) * (window.ndim - 1)
    result = jnp.broadcast_to(bias, (rows,) + bias.shape)
    for offset in range(taps):
        piece = window[offset : offset + rows].astype(jnp.float32)
        same = (window_ids[offset : offset + rows] == own_ids).reshape((rows,) + extra)
        result = result + jnp.where(same, piece * weight[offset].astype(jnp.float32), 0.0)
    return jax.nn.silu(result).astype(jnp.bfloat16)


def on_device(
    x_proj,
    bc_proj,
    z_proj,
    dt_raw,
    conv_x,
    conv_bc,
    bias_x,
    bias_bc,
    dt_bias,
    a_log,
    d_skip,
    norm_gain,
    seg_ids,
):
    tok_rows, inner_local = x_proj.shape
    heads_local = dt_raw.shape[1]
    state_size = STATE
    groups_local = bc_proj.shape[2] // state_size
    heads_group = heads_local // groups_local
    head_size = inner_local // heads_local
    block = STRETCH
    blocks = tok_rows // block
    margin = conv_x.shape[0] - 1
    bc_width = bc_proj.shape[1] * bc_proj.shape[2]
    rim = jnp.concatenate(
        [
            x_proj[tok_rows - margin :],
            bc_proj[tok_rows - margin :].reshape(margin, bc_width),
            jnp.broadcast_to(seg_ids[tok_rows - margin :, None].astype(jnp.bfloat16), (margin, 128)),
        ],
        axis=1,
    )
    rim = from_behind(rim, "seq", 1)
    rim_x = rim[:, :inner_local]
    rim_bc = rim[:, inner_local : inner_local + bc_width].reshape(margin, *bc_proj.shape[1:])
    rim_ids = rim[:, inner_local + bc_width]
    own_ids = seg_ids.astype(jnp.float32)
    window_ids = jnp.concatenate([rim_ids.astype(jnp.float32), own_ids])
    x_conv = causal_conv(jnp.concatenate([rim_x, x_proj]), window_ids, conv_x, bias_x, tok_rows)
    bc_conv = causal_conv(
        jnp.concatenate([rim_bc, bc_proj]), window_ids, conv_bc, bias_bc, tok_rows
    )
    step_size = jax.nn.softplus(dt_raw + dt_bias)
    log_decay = step_size * -jnp.exp(a_log)
    cumul = jnp.cumsum(log_decay.reshape(blocks, block, heads_local), axis=1)
    cum_heads = cumul.reshape(blocks, block, groups_local, heads_group).transpose(0, 2, 3, 1)
    step_heads = step_size.reshape(blocks, block, groups_local, heads_group).transpose(0, 2, 3, 1)
    block_ids = own_ids.reshape(blocks, block)
    before_ids = window_ids[margin - 1 : margin - 1 + tok_rows : block]
    b_in = bc_conv[:, 0].reshape(blocks, block, groups_local, state_size)
    c_out = bc_conv[:, 1].reshape(blocks, block, groups_local, state_size)
    lower = jnp.tril(jnp.ones((block, block), dtype=bool))
    same = (block_ids[:, :, None] == block_ids[:, None, :]) & lower
    scores = jnp.einsum("cqgn,csgn->cgqs", c_out, b_in, preferred_element_type=jnp.float32)
    same_heads = same[:, None, None]
    spread = cum_heads[..., :, None] - cum_heads[..., None, :]
    decay = jnp.where(same_heads, jnp.exp(jnp.where(same_heads, spread, 0.0)), 0.0)
    mixing = (scores[:, :, None] * decay * step_heads[..., None, :]).astype(jnp.bfloat16)
    x_heads = x_conv.reshape(blocks, block, groups_local, heads_group, head_size)
    y_intra = jnp.einsum("cghqs,csghp->cqghp", mixing, x_heads, preferred_element_type=jnp.float32)
    tail_same = (block_ids == block_ids[:, -1:]).astype(jnp.float32)[:, None, None, :]
    weights = jnp.exp(cum_heads[..., -1:] - cum_heads) * step_heads * tail_same
    b_weighted = (
        b_in.transpose(0, 2, 1, 3)[:, :, None].astype(jnp.float32) * weights[..., None]
    ).astype(jnp.bfloat16)
    increment = jnp.einsum(
        "cghsn,csghp->cghpn", b_weighted, x_heads, preferred_element_type=jnp.float32
    )
    carry_gain = (
        jnp.exp(cum_heads[..., -1])
        * (block_ids[:, -1] == before_ids).astype(jnp.float32)[:, None, None]
    )
    link = (
        jnp.exp(cum_heads)
        * (block_ids == before_ids[:, None]).astype(jnp.float32)[:, None, None, :]
    )
    c_float = c_out.astype(jnp.float32)

    def recur(start_state):
        stacked = []
        current = start_state
        for index in range(blocks):
            stacked.append(current)
            current = carry_gain[index][..., None, None] * current + increment[index]
        return (jnp.stack(stacked), current)

    empty = jnp.zeros((groups_local, heads_group, head_size, state_size), jnp.float32)
    zero_states, summary = recur(empty)
    device_gain = carry_gain[0] * carry_gain[1]
    skip = d_skip.reshape(groups_local, heads_group)[..., None]
    base = (y_intra + skip * x_heads.astype(jnp.float32)).reshape(tok_rows, inner_local)
    gate = jax.nn.silu(z_proj.astype(jnp.float32))
    entering, (early, gate) = entering_state(device_gain, summary, "seq", (base * gate, gate))
    states, _ = recur(entering)
    lanes = heads_group * head_size
    states_t = states.transpose(0, 1, 4, 2, 3).reshape(blocks, groups_local, state_size, lanes)
    product = jnp.einsum("cqgn,cgnk->cqgk", c_float, states_t, precision=lax.Precision.HIGHEST)
    product = product.reshape(blocks, block, groups_local, heads_group, head_size)
    y_inter = (product * link.transpose(0, 3, 1, 2)[..., None]).reshape(tok_rows, inner_local)
    gated = early + y_inter * gate
    squares = summed_over(jnp.sum(gated * gated, axis=-1), "tp")
    scale = lax.rsqrt(squares / (inner_local * lax.axis_size("tp")) + 1e-05)
    return (gated * scale[:, None] * norm_gain).astype(jnp.bfloat16)


def solution(mesh):
    in_specs = (
        P("seq", "tp"),
        P("seq", None, "tp"),
        P("seq", "tp"),
        P("seq", "tp"),
        P(None, "tp"),
        P(None, None, "tp"),
        P("tp"),
        P(None, "tp"),
        P("tp"),
        P("tp"),
        P("tp"),
        P("tp"),
        P("seq"),
    )
    out_specs = P("seq", "tp")
    return jax.shard_map(
        on_device, mesh=mesh, in_specs=in_specs, out_specs=out_specs, check_vma=False
    )
```

```python
import jax
import jax.numpy as jnp
from jax import lax
from jax.sharding import PartitionSpec as P

STATE = 128
STRETCH = 256


def from_behind(block, axis, distance):
    devices = range(lax.axis_size(axis))
    route = [(i - distance, i) for i in devices if i - distance in devices]
    return lax.ppermute(block, axis, route)


def shifted(block, axis, pairs):
    return lax.ppermute(block, axis, pairs)


def fold(earlier, later):
    gain_e, state_e = earlier
    gain_l, state_l = later
    return (gain_e * gain_l, gain_l[..., None, None] * state_e + state_l)


def pack(gain, state):
    lanes = state.shape[-1]
    flat = state.reshape(-1, lanes)
    row = jnp.zeros((8, lanes), state.dtype).at[0, : gain.size].set(gain.reshape(-1))
    return jnp.concatenate([flat, row])


def unpack(packed, gain_shape, state_shape):
    rows = packed.shape[0] - 8
    count = 1
    for size in gain_shape:
        count *= size
    return (packed[rows, :count].reshape(gain_shape), packed[:rows].reshape(state_shape))


def entering_state(gain, state, axis):
    count = lax.axis_size(axis)
    chips = count // 2
    shapes = (gain.shape, state.shape)
    own = (gain, state)
    pair = unpack(shifted(pack(*own), axis, [(2 * c, 2 * c + 1) for c in range(chips)]), *shapes)
    chip_total = fold(pair, own)
    for reach in (1, 2, 4):
        route = [(2 * c + 1, 2 * (c + reach) + 1) for c in range(chips - reach)]
        got = unpack(shifted(pack(*chip_total), axis, route), *shapes)
        chip_total = fold(got, chip_total)
    mine = lax.axis_index(axis)
    even = mine % 2 == 0
    split = state.shape[1] // 2
    prefix = chip_total[1]
    to_even = shifted(prefix[:, :split], axis, [(2 * c - 1, 2 * c) for c in range(1, chips)])
    to_odd = shifted(prefix[:, split:], axis, [(2 * c - 1, 2 * c + 1) for c in range(1, chips)])
    held = jnp.where(even, to_even, to_odd)
    swap = [(2 * c, 2 * c + 1) for c in range(chips)] + [(2 * c + 1, 2 * c) for c in range(chips)]
    other = shifted(held, axis, swap)
    behind = jnp.where(
        even,
        jnp.concatenate([held, other], axis=1),
        jnp.concatenate([other, held], axis=1),
    )
    odd_entering = pair[0][..., None, None] * behind + pair[1]
    return jnp.where(even, behind, odd_entering)


def summed_over(value, axis):
    count = lax.axis_size(axis)
    spread = jnp.broadcast_to(value[None], (count,) + value.shape)
    return lax.all_to_all(spread, axis, 0, 0, tiled=False).sum(0)


def causal_conv(window, window_ids, weight, bias, rows):
    taps = weight.shape[0]
    own_ids = window_ids[taps - 1 :]
    extra = (1,) * (window.ndim - 1)
    result = jnp.broadcast_to(bias, (rows,) + bias.shape)
    for offset in range(taps):
        piece = window[offset : offset + rows].astype(jnp.float32)
        same = (window_ids[offset : offset + rows] == own_ids).reshape((rows,) + extra)
        result = result + jnp.where(same, piece * weight[offset].astype(jnp.float32), 0.0)
    return jax.nn.silu(result).astype(jnp.bfloat16)


def on_device(
    x_proj,
    bc_proj,
    z_proj,
    dt_raw,
    conv_x,
    conv_bc,
    bias_x,
    bias_bc,
    dt_bias,
    a_log,
    d_skip,
    norm_gain,
    seg_ids,
):
    tok_rows, inner_local = x_proj.shape
    heads_local = dt_raw.shape[1]
    state_size = STATE
    groups_local = bc_proj.shape[2] // state_size
    heads_group = heads_local // groups_local
    head_size = inner_local // heads_local
    block = STRETCH
    blocks = tok_rows // block
    margin = conv_x.shape[0] - 1
    bc_width = bc_proj.shape[1] * bc_proj.shape[2]
    rim = jnp.concatenate(
        [
            x_proj[tok_rows - margin :],
            bc_proj[tok_rows - margin :].reshape(margin, bc_width),
            jnp.broadcast_to(seg_ids[tok_rows - margin :, None].astype(jnp.bfloat16), (margin, 128)),
        ],
        axis=1,
    )
    rim = from_behind(rim, "seq", 1)
    rim_x = rim[:, :inner_local]
    rim_bc = rim[:, inner_local : inner_local + bc_width].reshape(margin, *bc_proj.shape[1:])
    rim_ids = rim[:, inner_local + bc_width]
    own_ids = seg_ids.astype(jnp.float32)
    window_ids = jnp.concatenate([rim_ids.astype(jnp.float32), own_ids])
    x_conv = causal_conv(jnp.concatenate([rim_x, x_proj]), window_ids, conv_x, bias_x, tok_rows)
    bc_conv = causal_conv(
        jnp.concatenate([rim_bc, bc_proj]), window_ids, conv_bc, bias_bc, tok_rows
    )
    step_size = jax.nn.softplus(dt_raw + dt_bias)
    log_decay = step_size * -jnp.exp(a_log)
    cumul = jnp.cumsum(log_decay.reshape(blocks, block, heads_local), axis=1)
    cum_heads = cumul.reshape(blocks, block, groups_local, heads_group).transpose(0, 2, 3, 1)
    step_heads = step_size.reshape(blocks, block, groups_local, heads_group).transpose(0, 2, 3, 1)
    block_ids = own_ids.reshape(blocks, block)
    before_ids = window_ids[margin - 1 : margin - 1 + tok_rows : block]
    b_in = bc_conv[:, 0].reshape(blocks, block, groups_local, state_size)
    c_out = bc_conv[:, 1].reshape(blocks, block, groups_local, state_size)
    lower = jnp.tril(jnp.ones((block, block), dtype=bool))
    same = (block_ids[:, :, None] == block_ids[:, None, :]) & lower
    scores = jnp.einsum("cqgn,csgn->cgqs", c_out, b_in, preferred_element_type=jnp.float32)
    same_heads = same[:, None, None]
    spread = cum_heads[..., :, None] - cum_heads[..., None, :]
    decay = jnp.where(same_heads, jnp.exp(jnp.where(same_heads, spread, 0.0)), 0.0)
    mixing = (scores[:, :, None] * decay * step_heads[..., None, :]).astype(jnp.bfloat16)
    x_heads = x_conv.reshape(blocks, block, groups_local, heads_group, head_size)
    y_intra = jnp.einsum("cghqs,csghp->cqghp", mixing, x_heads, preferred_element_type=jnp.float32)
    tail_same = (block_ids == block_ids[:, -1:]).astype(jnp.float32)[:, None, None, :]
    weights = jnp.exp(cum_heads[..., -1:] - cum_heads) * step_heads * tail_same
    b_weighted = (
        b_in.transpose(0, 2, 1, 3)[:, :, None].astype(jnp.float32) * weights[..., None]
    ).astype(jnp.bfloat16)
    increment = jnp.einsum(
        "cghsn,csghp->cghpn", b_weighted, x_heads, preferred_element_type=jnp.float32
    )
    carry_gain = (
        jnp.exp(cum_heads[..., -1])
        * (block_ids[:, -1] == before_ids).astype(jnp.float32)[:, None, None]
    )
    link = (
        jnp.exp(cum_heads)
        * (block_ids == before_ids[:, None]).astype(jnp.float32)[:, None, None, :]
    )
    c_float = c_out.astype(jnp.float32)

    def recur(start_state):
        stacked = []
        current = start_state
        for index in range(blocks):
            stacked.append(current)
            current = carry_gain[index][..., None, None] * current + increment[index]
        return (jnp.stack(stacked), current)

    empty = jnp.zeros((groups_local, heads_group, head_size, state_size), jnp.float32)
    zero_states, summary = recur(empty)
    device_gain = carry_gain[0] * carry_gain[1]
    entering = entering_state(device_gain, summary, "seq")
    states, _ = recur(entering)
    product = jnp.einsum("cqgn,cghpn->cqghp", c_float, states, precision=lax.Precision.HIGHEST)
    y_inter = product * link.transpose(0, 3, 1, 2)[..., None]
    skip = d_skip.reshape(groups_local, heads_group)[..., None]
    mixed = y_intra + y_inter + skip * x_heads.astype(jnp.float32)
    gated = mixed.reshape(tok_rows, inner_local) * jax.nn.silu(z_proj.astype(jnp.float32))
    squares = summed_over(jnp.sum(gated * gated, axis=-1), "tp")
    scale = lax.rsqrt(squares / (inner_local * lax.axis_size("tp")) + 1e-05)
    return (gated * scale[:, None] * norm_gain).astype(jnp.bfloat16)


def solution(mesh):
    in_specs = (
        P("seq", "tp"),
        P("seq", None, "tp"),
        P("seq", "tp"),
        P("seq", "tp"),
        P(None, "tp"),
        P(None, None, "tp"),
        P("tp"),
        P(None, "tp"),
        P("tp"),
        P("tp"),
        P("tp"),
        P("tp"),
        P("seq"),
    )
    out_specs = P("seq", "tp")
    return jax.shard_map(
        on_device, mesh=mesh, in_specs=in_specs, out_specs=out_specs, check_vma=False
    )
```

```python
import jax
import jax.numpy as jnp
from jax import lax
from jax.sharding import PartitionSpec as P
from jax.experimental import pallas as pl

STATE = 128
STRETCH = 256


def from_behind(block, axis, distance):
    devices = range(lax.axis_size(axis))
    route = [(i - distance, i) for i in devices if i - distance in devices]
    return lax.ppermute(block, axis, route)


def shifted(block, axis, pairs):
    return lax.ppermute(block, axis, pairs)


def fold(earlier, later):
    gain_e, state_e = earlier
    gain_l, state_l = later
    return (gain_e * gain_l, gain_l[..., None, None] * state_e + state_l)


def pack(gain, state):
    lanes = state.shape[-1]
    flat = state.reshape(-1, lanes)
    row = jnp.zeros((8, lanes), state.dtype).at[0, : gain.size].set(gain.reshape(-1))
    return jnp.concatenate([flat, row])


def unpack(packed, gain_shape, state_shape):
    rows = packed.shape[0] - 8
    count = 1
    for size in gain_shape:
        count *= size
    return (packed[rows, :count].reshape(gain_shape), packed[:rows].reshape(state_shape))


def entering_state(gain, state, axis):
    count = lax.axis_size(axis)
    chips = count // 2
    shapes = (gain.shape, state.shape)
    own = (gain, state)
    pair = unpack(shifted(pack(*own), axis, [(2 * c, 2 * c + 1) for c in range(chips)]), *shapes)
    chip_total = fold(pair, own)
    for reach in (1, 2, 4):
        route = [(2 * c + 1, 2 * (c + reach) + 1) for c in range(chips - reach)]
        got = unpack(shifted(pack(*chip_total), axis, route), *shapes)
        chip_total = fold(got, chip_total)
    mine = lax.axis_index(axis)
    even = mine % 2 == 0
    split = state.shape[1] // 2
    prefix = chip_total[1]
    to_even = shifted(prefix[:, :split], axis, [(2 * c - 1, 2 * c) for c in range(1, chips)])
    to_odd = shifted(prefix[:, split:], axis, [(2 * c - 1, 2 * c + 1) for c in range(1, chips)])
    held = jnp.where(even, to_even, to_odd)
    swap = [(2 * c, 2 * c + 1) for c in range(chips)] + [(2 * c + 1, 2 * c) for c in range(chips)]
    other = shifted(held, axis, swap)
    behind = jnp.where(
        even,
        jnp.concatenate([held, other], axis=1),
        jnp.concatenate([other, held], axis=1),
    )
    odd_entering = pair[0][..., None, None] * behind + pair[1]
    return jnp.where(even, behind, odd_entering)


def summed_over(value, axis):
    count = lax.axis_size(axis)
    spread = jnp.broadcast_to(value[None], (count,) + value.shape)
    return lax.all_to_all(spread, axis, 0, 0, tiled=False).sum(0)


def tail_kernel(base_ref, z_ref, c_ref, s_ref, link_ref, expand_ref, gated_ref, ss_ref):
    state = s_ref[0]
    s_hi = state.astype(jnp.bfloat16)
    s_lo = (state - s_hi.astype(jnp.float32)).astype(jnp.bfloat16)
    c_row = c_ref[...]
    nt = (((1,), (1,)), ((), ()))
    product = lax.dot_general(c_row, s_hi, nt, preferred_element_type=jnp.float32)
    product = product + lax.dot_general(c_row, s_lo, nt, preferred_element_type=jnp.float32)
    link = link_ref[...]
    expand = expand_ref[...]
    l_hi = link.astype(jnp.bfloat16)
    rest = link - l_hi.astype(jnp.float32)
    l_mid = rest.astype(jnp.bfloat16)
    l_lo = (rest - l_mid.astype(jnp.float32)).astype(jnp.bfloat16)
    spread = jnp.dot(l_hi, expand, preferred_element_type=jnp.float32)
    spread = spread + jnp.dot(l_mid, expand, preferred_element_type=jnp.float32)
    spread = spread + jnp.dot(l_lo, expand, preferred_element_type=jnp.float32)
    z = z_ref[...].astype(jnp.float32)
    gate = z * (1.0 / (1.0 + jnp.exp(-z)))
    gated = (base_ref[...] + product * spread) * gate
    gated_ref[...] = gated
    ss_ref[...] = jnp.sum(gated * gated, axis=1, keepdims=True)


def gated_tail(base, z_proj, c_rows, states, link_rows, block):
    rows, width = base.shape
    heads = link_rows.shape[1]
    state_size = c_rows.shape[1]
    expand = jnp.repeat(jnp.eye(heads, dtype=jnp.bfloat16), width // heads, axis=1)
    flops = 2 * rows * width * (2 * state_size + 3 * heads)
    return pl.pallas_call(
        tail_kernel,
        grid=(rows // block,),
        in_specs=[
            pl.BlockSpec((block, width), lambda i: (i, 0)),
            pl.BlockSpec((block, width), lambda i: (i, 0)),
            pl.BlockSpec((block, state_size), lambda i: (i, 0)),
            pl.BlockSpec((1, width, state_size), lambda i: (i, 0, 0)),
            pl.BlockSpec((block, heads), lambda i: (i, 0)),
            pl.BlockSpec((heads, width), lambda i: (0, 0)),
        ],
        out_specs=[
            pl.BlockSpec((block, width), lambda i: (i, 0)),
            pl.BlockSpec((block, 1), lambda i: (i, 0)),
        ],
        out_shape=[
            jax.ShapeDtypeStruct((rows, width), jnp.float32),
            jax.ShapeDtypeStruct((rows, 1), jnp.float32),
        ],
        cost_estimate=pl.CostEstimate(
            flops=flops, transcendentals=rows * width, bytes_accessed=rows * width * 10
        ),
    )(base, z_proj, c_rows, states, link_rows, expand)


def causal_conv(window, window_ids, weight, bias, rows):
    taps = weight.shape[0]
    own_ids = window_ids[taps - 1 :]
    extra = (1,) * (window.ndim - 1)
    result = jnp.broadcast_to(bias, (rows,) + bias.shape)
    for offset in range(taps):
        piece = window[offset : offset + rows].astype(jnp.float32)
        same = (window_ids[offset : offset + rows] == own_ids).reshape((rows,) + extra)
        result = result + jnp.where(same, piece * weight[offset].astype(jnp.float32), 0.0)
    return jax.nn.silu(result).astype(jnp.bfloat16)


def on_device(
    x_proj,
    bc_proj,
    z_proj,
    dt_raw,
    conv_x,
    conv_bc,
    bias_x,
    bias_bc,
    dt_bias,
    a_log,
    d_skip,
    norm_gain,
    seg_ids,
):
    tok_rows, inner_local = x_proj.shape
    heads_local = dt_raw.shape[1]
    state_size = STATE
    groups_local = bc_proj.shape[2] // state_size
    heads_group = heads_local // groups_local
    head_size = inner_local // heads_local
    block = STRETCH
    blocks = tok_rows // block
    margin = conv_x.shape[0] - 1
    bc_width = bc_proj.shape[1] * bc_proj.shape[2]
    rim = jnp.concatenate(
        [
            x_proj[tok_rows - margin :],
            bc_proj[tok_rows - margin :].reshape(margin, bc_width),
            jnp.broadcast_to(seg_ids[tok_rows - margin :, None].astype(jnp.bfloat16), (margin, 128)),
        ],
        axis=1,
    )
    rim = from_behind(rim, "seq", 1)
    rim_x = rim[:, :inner_local]
    rim_bc = rim[:, inner_local : inner_local + bc_width].reshape(margin, *bc_proj.shape[1:])
    rim_ids = rim[:, inner_local + bc_width]
    own_ids = seg_ids.astype(jnp.float32)
    window_ids = jnp.concatenate([rim_ids.astype(jnp.float32), own_ids])
    x_conv = causal_conv(jnp.concatenate([rim_x, x_proj]), window_ids, conv_x, bias_x, tok_rows)
    bc_conv = causal_conv(
        jnp.concatenate([rim_bc, bc_proj]), window_ids, conv_bc, bias_bc, tok_rows
    )
    step_size = jax.nn.softplus(dt_raw + dt_bias)
    log_decay = step_size * -jnp.exp(a_log)
    cumul = jnp.cumsum(log_decay.reshape(blocks, block, heads_local), axis=1)
    cum_heads = cumul.reshape(blocks, block, groups_local, heads_group).transpose(0, 2, 3, 1)
    step_heads = step_size.reshape(blocks, block, groups_local, heads_group).transpose(0, 2, 3, 1)
    block_ids = own_ids.reshape(blocks, block)
    before_ids = window_ids[margin - 1 : margin - 1 + tok_rows : block]
    b_in = bc_conv[:, 0].reshape(blocks, block, groups_local, state_size)
    c_out = bc_conv[:, 1].reshape(blocks, block, groups_local, state_size)
    lower = jnp.tril(jnp.ones((block, block), dtype=bool))
    same = (block_ids[:, :, None] == block_ids[:, None, :]) & lower
    scores = jnp.einsum("cqgn,csgn->cgqs", c_out, b_in, preferred_element_type=jnp.float32)
    same_heads = same[:, None, None]
    spread = cum_heads[..., :, None] - cum_heads[..., None, :]
    decay = jnp.where(same_heads, jnp.exp(jnp.where(same_heads, spread, 0.0)), 0.0)
    mixing = (scores[:, :, None] * decay * step_heads[..., None, :]).astype(jnp.bfloat16)
    x_heads = x_conv.reshape(blocks, block, groups_local, heads_group, head_size)
    y_intra = jnp.einsum("cghqs,csghp->cqghp", mixing, x_heads, preferred_element_type=jnp.float32)
    tail_same = (block_ids == block_ids[:, -1:]).astype(jnp.float32)[:, None, None, :]
    weights = jnp.exp(cum_heads[..., -1:] - cum_heads) * step_heads * tail_same
    b_weighted = (
        b_in.transpose(0, 2, 1, 3)[:, :, None].astype(jnp.float32) * weights[..., None]
    ).astype(jnp.bfloat16)
    increment = jnp.einsum(
        "cghsn,csghp->cghpn", b_weighted, x_heads, preferred_element_type=jnp.float32
    )
    carry_gain = (
        jnp.exp(cum_heads[..., -1])
        * (block_ids[:, -1] == before_ids).astype(jnp.float32)[:, None, None]
    )
    link = (
        jnp.exp(cum_heads)
        * (block_ids == before_ids[:, None]).astype(jnp.float32)[:, None, None, :]
    )

    def recur(start_state):
        stacked = []
        current = start_state
        for index in range(blocks):
            stacked.append(current)
            current = carry_gain[index][..., None, None] * current + increment[index]
        return (jnp.stack(stacked), current)

    empty = jnp.zeros((groups_local, heads_group, head_size, state_size), jnp.float32)
    zero_states, summary = recur(empty)
    device_gain = carry_gain[0] * carry_gain[1]
    entering = entering_state(device_gain, summary, "seq")
    states, _ = recur(entering)
    skip = d_skip.reshape(groups_local, heads_group)[..., None]
    base = (y_intra + skip * x_heads.astype(jnp.float32)).reshape(tok_rows, inner_local)
    link_rows = link.transpose(0, 3, 1, 2).reshape(tok_rows, heads_local)
    gated, sums = gated_tail(
        base,
        z_proj,
        c_out.reshape(tok_rows, state_size),
        states.reshape(blocks, heads_local * head_size, state_size),
        link_rows,
        block,
    )
    squares = summed_over(sums[:, 0], "tp")
    scale = lax.rsqrt(squares / (inner_local * lax.axis_size("tp")) + 1e-05)
    return (gated * scale[:, None] * norm_gain).astype(jnp.bfloat16)


def solution(mesh):
    in_specs = (
        P("seq", "tp"),
        P("seq", None, "tp"),
        P("seq", "tp"),
        P("seq", "tp"),
        P(None, "tp"),
        P(None, None, "tp"),
        P("tp"),
        P(None, "tp"),
        P("tp"),
        P("tp"),
        P("tp"),
        P("tp"),
        P("seq"),
    )
    out_specs = P("seq", "tp")
    return jax.shard_map(
        on_device, mesh=mesh, in_specs=in_specs, out_specs=out_specs, check_vma=False
    )
```

```python
import jax
import jax.numpy as jnp
from jax import lax
from jax.sharding import PartitionSpec as P

STATE = 128
STRETCH = 256


def from_behind(block, axis, distance):
    devices = range(lax.axis_size(axis))
    route = [(i - distance, i) for i in devices if i - distance in devices]
    return lax.ppermute(block, axis, route)


def shifted(block, axis, pairs):
    return lax.ppermute(block, axis, pairs)


def fold(earlier, later):
    gain_e, state_e = earlier
    gain_l, state_l = later
    return (gain_e * gain_l, gain_l[..., None, None] * state_e + state_l)


def pack(gain, state):
    lanes = state.shape[-1]
    flat = state.reshape(-1, lanes)
    row = jnp.zeros((8, lanes), state.dtype).at[0, : gain.size].set(gain.reshape(-1))
    return jnp.concatenate([flat, row])


def unpack(packed, gain_shape, state_shape):
    rows = packed.shape[0] - 8
    count = 1
    for size in gain_shape:
        count *= size
    return (packed[rows, :count].reshape(gain_shape), packed[:rows].reshape(state_shape))


def entering_state(gain, state, axis):
    count = lax.axis_size(axis)
    chips = count // 2
    shapes = (gain.shape, state.shape)
    own = (gain, state)
    pair = unpack(shifted(pack(*own), axis, [(2 * c, 2 * c + 1) for c in range(chips)]), *shapes)
    chip_total = fold(pair, own)
    for reach in (1, 2):
        route = [(2 * c + 1, 2 * (c + reach) + 1) for c in range(chips - reach)]
        got = unpack(shifted(pack(*chip_total), axis, route), *shapes)
        chip_total = fold(got, chip_total)
    far = 5
    mine = lax.axis_index(axis)
    even = mine % 2 == 0
    split = state.shape[1] // 2
    gain_t, state_t = chip_total
    halves = ((gain.shape[0], split), (state.shape[0], split) + state.shape[2:])
    near_lo = shifted(
        pack(gain_t[:, :split], state_t[:, :split]), axis, [(2 * c - 1, 2 * c) for c in range(1, chips)]
    )
    near_hi = shifted(
        pack(gain_t[:, split:], state_t[:, split:]), axis, [(2 * c - 1, 2 * c + 1) for c in range(1, chips)]
    )
    far_lo = shifted(
        state_t[:, :split], axis, [(2 * (c - far) + 1, 2 * c) for c in range(far, chips)]
    )
    far_hi = shifted(
        state_t[:, split:], axis, [(2 * (c - far) + 1, 2 * c + 1) for c in range(far, chips)]
    )
    near_gain, near_state = unpack(jnp.where(even, near_lo, near_hi), *halves)
    held = near_gain[..., None, None] * jnp.where(even, far_lo, far_hi) + near_state
    swap = [(2 * c, 2 * c + 1) for c in range(chips)] + [(2 * c + 1, 2 * c) for c in range(chips)]
    other = shifted(held, axis, swap)
    behind = jnp.where(
        even,
        jnp.concatenate([held, other], axis=1),
        jnp.concatenate([other, held], axis=1),
    )
    odd_entering = pair[0][..., None, None] * behind + pair[1]
    return jnp.where(even, behind, odd_entering)


def summed_over(value, axis):
    count = lax.axis_size(axis)
    spread = jnp.broadcast_to(value[None], (count,) + value.shape)
    return lax.all_to_all(spread, axis, 0, 0, tiled=False).sum(0)


def causal_conv(window, window_ids, weight, bias, rows):
    taps = weight.shape[0]
    own_ids = window_ids[taps - 1 :]
    extra = (1,) * (window.ndim - 1)
    result = jnp.broadcast_to(bias, (rows,) + bias.shape)
    for offset in range(taps):
        piece = window[offset : offset + rows].astype(jnp.float32)
        same = (window_ids[offset : offset + rows] == own_ids).reshape((rows,) + extra)
        result = result + jnp.where(same, piece * weight[offset].astype(jnp.float32), 0.0)
    return jax.nn.silu(result).astype(jnp.bfloat16)


def on_device(
    x_proj,
    bc_proj,
    z_proj,
    dt_raw,
    conv_x,
    conv_bc,
    bias_x,
    bias_bc,
    dt_bias,
    a_log,
    d_skip,
    norm_gain,
    seg_ids,
):
    tok_rows, inner_local = x_proj.shape
    heads_local = dt_raw.shape[1]
    state_size = STATE
    groups_local = bc_proj.shape[2] // state_size
    heads_group = heads_local // groups_local
    head_size = inner_local // heads_local
    block = STRETCH
    blocks = tok_rows // block
    margin = conv_x.shape[0] - 1
    bc_width = bc_proj.shape[1] * bc_proj.shape[2]
    rim = jnp.concatenate(
        [
            x_proj[tok_rows - margin :],
            bc_proj[tok_rows - margin :].reshape(margin, bc_width),
            jnp.broadcast_to(seg_ids[tok_rows - margin :, None].astype(jnp.bfloat16), (margin, 128)),
        ],
        axis=1,
    )
    rim = from_behind(rim, "seq", 1)
    rim_x = rim[:, :inner_local]
    rim_bc = rim[:, inner_local : inner_local + bc_width].reshape(margin, *bc_proj.shape[1:])
    rim_ids = rim[:, inner_local + bc_width]
    own_ids = seg_ids.astype(jnp.float32)
    window_ids = jnp.concatenate([rim_ids.astype(jnp.float32), own_ids])
    x_conv = causal_conv(jnp.concatenate([rim_x, x_proj]), window_ids, conv_x, bias_x, tok_rows)
    bc_conv = causal_conv(
        jnp.concatenate([rim_bc, bc_proj]), window_ids, conv_bc, bias_bc, tok_rows
    )
    step_size = jax.nn.softplus(dt_raw + dt_bias)
    log_decay = step_size * -jnp.exp(a_log)
    cumul = jnp.cumsum(log_decay.reshape(blocks, block, heads_local), axis=1)
    cum_heads = cumul.reshape(blocks, block, groups_local, heads_group).transpose(0, 2, 3, 1)
    step_heads = step_size.reshape(blocks, block, groups_local, heads_group).transpose(0, 2, 3, 1)
    block_ids = own_ids.reshape(blocks, block)
    before_ids = window_ids[margin - 1 : margin - 1 + tok_rows : block]
    b_in = bc_conv[:, 0].reshape(blocks, block, groups_local, state_size)
    c_out = bc_conv[:, 1].reshape(blocks, block, groups_local, state_size)
    lower = jnp.tril(jnp.ones((block, block), dtype=bool))
    same = (block_ids[:, :, None] == block_ids[:, None, :]) & lower
    scores = jnp.einsum("cqgn,csgn->cgqs", c_out, b_in, preferred_element_type=jnp.float32)
    same_heads = same[:, None, None]
    spread = cum_heads[..., :, None] - cum_heads[..., None, :]
    decay = jnp.where(same_heads, jnp.exp(jnp.where(same_heads, spread, 0.0)), 0.0)
    mixing = (scores[:, :, None] * decay * step_heads[..., None, :]).astype(jnp.bfloat16)
    x_heads = x_conv.reshape(blocks, block, groups_local, heads_group, head_size)
    y_intra = jnp.einsum("cghqs,csghp->cqghp", mixing, x_heads, preferred_element_type=jnp.float32)
    tail_same = (block_ids == block_ids[:, -1:]).astype(jnp.float32)[:, None, None, :]
    weights = jnp.exp(cum_heads[..., -1:] - cum_heads) * step_heads * tail_same
    b_weighted = (
        b_in.transpose(0, 2, 1, 3)[:, :, None].astype(jnp.float32) * weights[..., None]
    ).astype(jnp.bfloat16)
    increment = jnp.einsum(
        "cghsn,csghp->cghpn", b_weighted, x_heads, preferred_element_type=jnp.float32
    )
    carry_gain = (
        jnp.exp(cum_heads[..., -1])
        * (block_ids[:, -1] == before_ids).astype(jnp.float32)[:, None, None]
    )
    link = (
        jnp.exp(cum_heads)
        * (block_ids == before_ids[:, None]).astype(jnp.float32)[:, None, None, :]
    )
    c_float = c_out.astype(jnp.float32)

    def recur(start_state):
        stacked = []
        current = start_state
        for index in range(blocks):
            stacked.append(current)
            current = carry_gain[index][..., None, None] * current + increment[index]
        return (jnp.stack(stacked), current)

    empty = jnp.zeros((groups_local, heads_group, head_size, state_size), jnp.float32)
    zero_states, summary = recur(empty)
    device_gain = carry_gain[0] * carry_gain[1]
    entering = entering_state(device_gain, summary, "seq")
    states, _ = recur(entering)
    product = jnp.einsum("cqgn,cghpn->cqghp", c_float, states, precision=lax.Precision.HIGHEST)
    y_inter = product * link.transpose(0, 3, 1, 2)[..., None]
    skip = d_skip.reshape(groups_local, heads_group)[..., None]
    mixed = y_intra + y_inter + skip * x_heads.astype(jnp.float32)
    gated = mixed.reshape(tok_rows, inner_local) * jax.nn.silu(z_proj.astype(jnp.float32))
    squares = summed_over(jnp.sum(gated * gated, axis=-1), "tp")
    scale = lax.rsqrt(squares / (inner_local * lax.axis_size("tp")) + 1e-05)
    return (gated * scale[:, None] * norm_gain).astype(jnp.bfloat16)


def solution(mesh):
    in_specs = (
        P("seq", "tp"),
        P("seq", None, "tp"),
        P("seq", "tp"),
        P("seq", "tp"),
        P(None, "tp"),
        P(None, None, "tp"),
        P("tp"),
        P(None, "tp"),
        P("tp"),
        P("tp"),
        P("tp"),
        P("tp"),
        P("seq"),
    )
    out_specs = P("seq", "tp")
    return jax.shard_map(
        on_device, mesh=mesh, in_specs=in_specs, out_specs=out_specs, check_vma=False
    )
```

```python
import jax
import jax.numpy as jnp
from jax import lax
from jax.sharding import PartitionSpec as P

STATE = 128
STRETCH = 256


def from_behind(block, axis, distance):
    devices = range(lax.axis_size(axis))
    route = [(i - distance, i) for i in devices if i - distance in devices]
    return lax.ppermute(block, axis, route)


def shifted(block, axis, pairs):
    return lax.ppermute(block, axis, pairs)


def fold(earlier, later):
    gain_e, state_e = earlier
    gain_l, state_l = later
    return (gain_e * gain_l, gain_l[..., None, None] * state_e + state_l)


def pack(gain, state):
    lanes = state.shape[-1]
    flat = state.reshape(-1, lanes)
    row = jnp.zeros((8, lanes), state.dtype).at[0, : gain.size].set(gain.reshape(-1))
    return jnp.concatenate([flat, row])


def unpack(packed, gain_shape, state_shape):
    rows = packed.shape[0] - 8
    count = 1
    for size in gain_shape:
        count *= size
    return (packed[rows, :count].reshape(gain_shape), packed[:rows].reshape(state_shape))


def entering_state(gain, state, axis):
    count = lax.axis_size(axis)
    chips = count // 2
    shapes = (gain.shape, state.shape)
    own = (gain, state)
    pair = unpack(shifted(pack(*own), axis, [(2 * c, 2 * c + 1) for c in range(chips)]), *shapes)
    chip_total = fold(pair, own)
    for reach in (1, 2):
        route = [(2 * c + 1, 2 * (c + reach) + 1) for c in range(chips - reach)]
        got = unpack(shifted(pack(*chip_total), axis, route), *shapes)
        chip_total = fold(got, chip_total)
    far = 5
    mine = lax.axis_index(axis)
    even = mine % 2 == 0
    gain_t, state_t = chip_total
    far_state = shifted(state_t, axis, [(2 * (c - far) + 1, 2 * c + 1) for c in range(far, chips)])
    near = shifted(pack(*chip_total), axis, [(2 * c - 1, 2 * c) for c in range(1, chips)])
    held = jnp.where(even, near, pack(gain_t, far_state))
    swap = [(2 * c, 2 * c + 1) for c in range(chips)] + [(2 * c + 1, 2 * c) for c in range(chips)]
    other = shifted(held, axis, swap)
    near_gain, near_state = unpack(jnp.where(even, held, other), *shapes)
    _, far_got = unpack(jnp.where(even, other, held), *shapes)
    behind = near_gain[..., None, None] * far_got + near_state
    odd_entering = pair[0][..., None, None] * behind + pair[1]
    return jnp.where(even, behind, odd_entering)


def summed_over(value, axis):
    count = lax.axis_size(axis)
    spread = jnp.broadcast_to(value[None], (count,) + value.shape)
    return lax.all_to_all(spread, axis, 0, 0, tiled=False).sum(0)


def causal_conv(window, window_ids, weight, bias, rows):
    taps = weight.shape[0]
    own_ids = window_ids[taps - 1 :]
    extra = (1,) * (window.ndim - 1)
    result = jnp.broadcast_to(bias, (rows,) + bias.shape)
    for offset in range(taps):
        piece = window[offset : offset + rows].astype(jnp.float32)
        same = (window_ids[offset : offset + rows] == own_ids).reshape((rows,) + extra)
        result = result + jnp.where(same, piece * weight[offset].astype(jnp.float32), 0.0)
    return jax.nn.silu(result).astype(jnp.bfloat16)


def on_device(
    x_proj,
    bc_proj,
    z_proj,
    dt_raw,
    conv_x,
    conv_bc,
    bias_x,
    bias_bc,
    dt_bias,
    a_log,
    d_skip,
    norm_gain,
    seg_ids,
):
    tok_rows, inner_local = x_proj.shape
    heads_local = dt_raw.shape[1]
    state_size = STATE
    groups_local = bc_proj.shape[2] // state_size
    heads_group = heads_local // groups_local
    head_size = inner_local // heads_local
    block = STRETCH
    blocks = tok_rows // block
    margin = conv_x.shape[0] - 1
    bc_width = bc_proj.shape[1] * bc_proj.shape[2]
    rim = jnp.concatenate(
        [
            x_proj[tok_rows - margin :],
            bc_proj[tok_rows - margin :].reshape(margin, bc_width),
            jnp.broadcast_to(seg_ids[tok_rows - margin :, None].astype(jnp.bfloat16), (margin, 128)),
        ],
        axis=1,
    )
    rim = from_behind(rim, "seq", 1)
    rim_x = rim[:, :inner_local]
    rim_bc = rim[:, inner_local : inner_local + bc_width].reshape(margin, *bc_proj.shape[1:])
    rim_ids = rim[:, inner_local + bc_width]
    own_ids = seg_ids.astype(jnp.float32)
    window_ids = jnp.concatenate([rim_ids.astype(jnp.float32), own_ids])
    x_conv = causal_conv(jnp.concatenate([rim_x, x_proj]), window_ids, conv_x, bias_x, tok_rows)
    bc_conv = causal_conv(
        jnp.concatenate([rim_bc, bc_proj]), window_ids, conv_bc, bias_bc, tok_rows
    )
    step_size = jax.nn.softplus(dt_raw + dt_bias)
    log_decay = step_size * -jnp.exp(a_log)
    cumul = jnp.cumsum(log_decay.reshape(blocks, block, heads_local), axis=1)
    cum_heads = cumul.reshape(blocks, block, groups_local, heads_group).transpose(0, 2, 3, 1)
    step_heads = step_size.reshape(blocks, block, groups_local, heads_group).transpose(0, 2, 3, 1)
    block_ids = own_ids.reshape(blocks, block)
    before_ids = window_ids[margin - 1 : margin - 1 + tok_rows : block]
    b_in = bc_conv[:, 0].reshape(blocks, block, groups_local, state_size)
    c_out = bc_conv[:, 1].reshape(blocks, block, groups_local, state_size)
    lower = jnp.tril(jnp.ones((block, block), dtype=bool))
    same = (block_ids[:, :, None] == block_ids[:, None, :]) & lower
    scores = jnp.einsum("cqgn,csgn->cgqs", c_out, b_in, preferred_element_type=jnp.float32)
    same_heads = same[:, None, None]
    spread = cum_heads[..., :, None] - cum_heads[..., None, :]
    decay = jnp.where(same_heads, jnp.exp(jnp.where(same_heads, spread, 0.0)), 0.0)
    mixing = (scores[:, :, None] * decay * step_heads[..., None, :]).astype(jnp.bfloat16)
    x_heads = x_conv.reshape(blocks, block, groups_local, heads_group, head_size)
    y_intra = jnp.einsum("cghqs,csghp->cqghp", mixing, x_heads, preferred_element_type=jnp.float32)
    tail_same = (block_ids == block_ids[:, -1:]).astype(jnp.float32)[:, None, None, :]
    weights = jnp.exp(cum_heads[..., -1:] - cum_heads) * step_heads * tail_same
    b_weighted = (
        b_in.transpose(0, 2, 1, 3)[:, :, None].astype(jnp.float32) * weights[..., None]
    ).astype(jnp.bfloat16)
    increment = jnp.einsum(
        "cghsn,csghp->cghpn", b_weighted, x_heads, preferred_element_type=jnp.float32
    )
    carry_gain = (
        jnp.exp(cum_heads[..., -1])
        * (block_ids[:, -1] == before_ids).astype(jnp.float32)[:, None, None]
    )
    link = (
        jnp.exp(cum_heads)
        * (block_ids == before_ids[:, None]).astype(jnp.float32)[:, None, None, :]
    )
    c_float = c_out.astype(jnp.float32)

    def recur(start_state):
        stacked = []
        current = start_state
        for index in range(blocks):
            stacked.append(current)
            current = carry_gain[index][..., None, None] * current + increment[index]
        return (jnp.stack(stacked), current)

    empty = jnp.zeros((groups_local, heads_group, head_size, state_size), jnp.float32)
    zero_states, summary = recur(empty)
    device_gain = carry_gain[0] * carry_gain[1]
    entering = entering_state(device_gain, summary, "seq")
    states, _ = recur(entering)
    product = jnp.einsum("cqgn,cghpn->cqghp", c_float, states, precision=lax.Precision.HIGHEST)
    y_inter = product * link.transpose(0, 3, 1, 2)[..., None]
    skip = d_skip.reshape(groups_local, heads_group)[..., None]
    mixed = y_intra + y_inter + skip * x_heads.astype(jnp.float32)
    gated = mixed.reshape(tok_rows, inner_local) * jax.nn.silu(z_proj.astype(jnp.float32))
    squares = summed_over(jnp.sum(gated * gated, axis=-1), "tp")
    scale = lax.rsqrt(squares / (inner_local * lax.axis_size("tp")) + 1e-05)
    return (gated * scale[:, None] * norm_gain).astype(jnp.bfloat16)


def solution(mesh):
    in_specs = (
        P("seq", "tp"),
        P("seq", None, "tp"),
        P("seq", "tp"),
        P("seq", "tp"),
        P(None, "tp"),
        P(None, None, "tp"),
        P("tp"),
        P(None, "tp"),
        P("tp"),
        P("tp"),
        P("tp"),
        P("tp"),
        P("seq"),
    )
    out_specs = P("seq", "tp")
    return jax.shard_map(
        on_device, mesh=mesh, in_specs=in_specs, out_specs=out_specs, check_vma=False
    )
```

```python
import jax
import jax.numpy as jnp
from jax import lax
from jax.sharding import PartitionSpec as P

STATE = 128
STRETCH = 256


def from_behind(block, axis, distance):
    devices = range(lax.axis_size(axis))
    route = [(i - distance, i) for i in devices if i - distance in devices]
    return lax.ppermute(block, axis, route)


def shifted(block, axis, pairs):
    return lax.ppermute(block, axis, pairs)


def fold(earlier, later):
    gain_e, state_e = earlier
    gain_l, state_l = later
    return (gain_e * gain_l, gain_l[..., None, None] * state_e + state_l)


def pack(gain, state):
    lanes = state.shape[-1]
    flat = state.reshape(-1, lanes)
    row = jnp.zeros((8, lanes), state.dtype).at[0, : gain.size].set(gain.reshape(-1))
    return jnp.concatenate([flat, row])


def unpack(packed, gain_shape, state_shape):
    rows = packed.shape[0] - 8
    count = 1
    for size in gain_shape:
        count *= size
    return (packed[rows, :count].reshape(gain_shape), packed[:rows].reshape(state_shape))


def entering_state(gain, state, axis):
    count = lax.axis_size(axis)
    chips = count // 2
    shapes = (gain.shape, state.shape)
    own = (gain, state)
    pair = unpack(shifted(pack(*own), axis, [(2 * c, 2 * c + 1) for c in range(chips)]), *shapes)
    chip_total = fold(pair, own)
    route = [(2 * c + 1, 2 * (c + 1) + 1) for c in range(chips - 1)]
    chip_total = fold(unpack(shifted(pack(*chip_total), axis, route), *shapes), chip_total)
    mine = lax.axis_index(axis)
    even = mine % 2 == 0
    packed = pack(*chip_total)

    def fetch(value, back, core):
        return shifted(value, axis, [(2 * (c - back) + 1, 2 * c + core) for c in range(back, chips)])

    far_last = unpack(fetch(packed, 7, 1), *shapes)
    far_next = unpack(fetch(packed, 5, 1), *shapes)
    near_last = unpack(fetch(packed, 3, 0), *shapes)
    near_next = unpack(fetch(packed, 1, 0), *shapes)
    near = fold(near_last, near_next)
    far = fold(far_last, far_next)
    held = jnp.where(even, pack(*near), pack(*far))
    swap = [(2 * c, 2 * c + 1) for c in range(chips)] + [(2 * c + 1, 2 * c) for c in range(chips)]
    other = shifted(held, axis, swap)
    near_gain, near_state = unpack(jnp.where(even, held, other), *shapes)
    _, far_state = unpack(jnp.where(even, other, held), *shapes)
    behind = near_gain[..., None, None] * far_state + near_state
    odd_entering = pair[0][..., None, None] * behind + pair[1]
    return jnp.where(even, behind, odd_entering)


def summed_over(value, axis):
    count = lax.axis_size(axis)
    spread = jnp.broadcast_to(value[None], (count,) + value.shape)
    return lax.all_to_all(spread, axis, 0, 0, tiled=False).sum(0)


def causal_conv(window, window_ids, weight, bias, rows):
    taps = weight.shape[0]
    own_ids = window_ids[taps - 1 :]
    extra = (1,) * (window.ndim - 1)
    result = jnp.broadcast_to(bias, (rows,) + bias.shape)
    for offset in range(taps):
        piece = window[offset : offset + rows].astype(jnp.float32)
        same = (window_ids[offset : offset + rows] == own_ids).reshape((rows,) + extra)
        result = result + jnp.where(same, piece * weight[offset].astype(jnp.float32), 0.0)
    return jax.nn.silu(result).astype(jnp.bfloat16)


def on_device(
    x_proj,
    bc_proj,
    z_proj,
    dt_raw,
    conv_x,
    conv_bc,
    bias_x,
    bias_bc,
    dt_bias,
    a_log,
    d_skip,
    norm_gain,
    seg_ids,
):
    tok_rows, inner_local = x_proj.shape
    heads_local = dt_raw.shape[1]
    state_size = STATE
    groups_local = bc_proj.shape[2] // state_size
    heads_group = heads_local // groups_local
    head_size = inner_local // heads_local
    block = STRETCH
    blocks = tok_rows // block
    margin = conv_x.shape[0] - 1
    bc_width = bc_proj.shape[1] * bc_proj.shape[2]
    rim = jnp.concatenate(
        [
            x_proj[tok_rows - margin :],
            bc_proj[tok_rows - margin :].reshape(margin, bc_width),
            jnp.broadcast_to(seg_ids[tok_rows - margin :, None].astype(jnp.bfloat16), (margin, 128)),
        ],
        axis=1,
    )
    rim = from_behind(rim, "seq", 1)
    rim_x = rim[:, :inner_local]
    rim_bc = rim[:, inner_local : inner_local + bc_width].reshape(margin, *bc_proj.shape[1:])
    rim_ids = rim[:, inner_local + bc_width]
    own_ids = seg_ids.astype(jnp.float32)
    window_ids = jnp.concatenate([rim_ids.astype(jnp.float32), own_ids])
    x_conv = causal_conv(jnp.concatenate([rim_x, x_proj]), window_ids, conv_x, bias_x, tok_rows)
    bc_conv = causal_conv(
        jnp.concatenate([rim_bc, bc_proj]), window_ids, conv_bc, bias_bc, tok_rows
    )
    step_size = jax.nn.softplus(dt_raw + dt_bias)
    log_decay = step_size * -jnp.exp(a_log)
    cumul = jnp.cumsum(log_decay.reshape(blocks, block, heads_local), axis=1)
    cum_heads = cumul.reshape(blocks, block, groups_local, heads_group).transpose(0, 2, 3, 1)
    step_heads = step_size.reshape(blocks, block, groups_local, heads_group).transpose(0, 2, 3, 1)
    block_ids = own_ids.reshape(blocks, block)
    before_ids = window_ids[margin - 1 : margin - 1 + tok_rows : block]
    b_in = bc_conv[:, 0].reshape(blocks, block, groups_local, state_size)
    c_out = bc_conv[:, 1].reshape(blocks, block, groups_local, state_size)
    lower = jnp.tril(jnp.ones((block, block), dtype=bool))
    same = (block_ids[:, :, None] == block_ids[:, None, :]) & lower
    scores = jnp.einsum("cqgn,csgn->cgqs", c_out, b_in, preferred_element_type=jnp.float32)
    same_heads = same[:, None, None]
    spread = cum_heads[..., :, None] - cum_heads[..., None, :]
    decay = jnp.where(same_heads, jnp.exp(jnp.where(same_heads, spread, 0.0)), 0.0)
    mixing = (scores[:, :, None] * decay * step_heads[..., None, :]).astype(jnp.bfloat16)
    x_heads = x_conv.reshape(blocks, block, groups_local, heads_group, head_size)
    y_intra = jnp.einsum("cghqs,csghp->cqghp", mixing, x_heads, preferred_element_type=jnp.float32)
    tail_same = (block_ids == block_ids[:, -1:]).astype(jnp.float32)[:, None, None, :]
    weights = jnp.exp(cum_heads[..., -1:] - cum_heads) * step_heads * tail_same
    b_weighted = (
        b_in.transpose(0, 2, 1, 3)[:, :, None].astype(jnp.float32) * weights[..., None]
    ).astype(jnp.bfloat16)
    increment = jnp.einsum(
        "cghsn,csghp->cghpn", b_weighted, x_heads, preferred_element_type=jnp.float32
    )
    carry_gain = (
        jnp.exp(cum_heads[..., -1])
        * (block_ids[:, -1] == before_ids).astype(jnp.float32)[:, None, None]
    )
    link = (
        jnp.exp(cum_heads)
        * (block_ids == before_ids[:, None]).astype(jnp.float32)[:, None, None, :]
    )
    c_float = c_out.astype(jnp.float32)

    def recur(start_state):
        stacked = []
        current = start_state
        for index in range(blocks):
            stacked.append(current)
            current = carry_gain[index][..., None, None] * current + increment[index]
        return (jnp.stack(stacked), current)

    empty = jnp.zeros((groups_local, heads_group, head_size, state_size), jnp.float32)
    zero_states, summary = recur(empty)
    device_gain = carry_gain[0] * carry_gain[1]
    entering = entering_state(device_gain, summary, "seq")
    states, _ = recur(entering)
    product = jnp.einsum("cqgn,cghpn->cqghp", c_float, states, precision=lax.Precision.HIGHEST)
    y_inter = product * link.transpose(0, 3, 1, 2)[..., None]
    skip = d_skip.reshape(groups_local, heads_group)[..., None]
    mixed = y_intra + y_inter + skip * x_heads.astype(jnp.float32)
    gated = mixed.reshape(tok_rows, inner_local) * jax.nn.silu(z_proj.astype(jnp.float32))
    squares = summed_over(jnp.sum(gated * gated, axis=-1), "tp")
    scale = lax.rsqrt(squares / (inner_local * lax.axis_size("tp")) + 1e-05)
    return (gated * scale[:, None] * norm_gain).astype(jnp.bfloat16)


def solution(mesh):
    in_specs = (
        P("seq", "tp"),
        P("seq", None, "tp"),
        P("seq", "tp"),
        P("seq", "tp"),
        P(None, "tp"),
        P(None, None, "tp"),
        P("tp"),
        P(None, "tp"),
        P("tp"),
        P("tp"),
        P("tp"),
        P("tp"),
        P("seq"),
    )
    out_specs = P("seq", "tp")
    return jax.shard_map(
        on_device, mesh=mesh, in_specs=in_specs, out_specs=out_specs, check_vma=False
    )
```

```python
import jax
import jax.numpy as jnp
from jax import lax
from jax.sharding import PartitionSpec as P

STATE = 128
STRETCH = 256


def from_behind(block, axis, distance):
    devices = range(lax.axis_size(axis))
    route = [(i - distance, i) for i in devices if i - distance in devices]
    return lax.ppermute(block, axis, route)


def shifted(block, axis, pairs):
    return lax.ppermute(block, axis, pairs)


def fold(earlier, later):
    gain_e, state_e = earlier
    gain_l, state_l = later
    return (gain_e * gain_l, gain_l[..., None, None] * state_e + state_l)


def pack(gain, state):
    lanes = state.shape[-1]
    flat = state.reshape(-1, lanes)
    row = jnp.zeros((8, lanes), state.dtype).at[0, : gain.size].set(gain.reshape(-1))
    return jnp.concatenate([flat, row])


def unpack(packed, gain_shape, state_shape):
    rows = packed.shape[0] - 8
    count = 1
    for size in gain_shape:
        count *= size
    return (packed[rows, :count].reshape(gain_shape), packed[:rows].reshape(state_shape))


def entering_state(gain, state, axis, ride):
    count = lax.axis_size(axis)
    chips = count // 2
    shapes = (gain.shape, state.shape)
    own = (gain, state)
    pair = unpack(shifted(pack(*own), axis, [(2 * c, 2 * c + 1) for c in range(chips)]), *shapes)
    chip_total = fold(pair, own)
    route = [(2 * c + 1, 2 * (c + 1) + 1) for c in range(chips - 1)]
    chip_total = fold(unpack(shifted(pack(*chip_total), axis, route), *shapes), chip_total)
    mine = lax.axis_index(axis)
    even = mine % 2 == 0
    packed = pack(*chip_total)

    def fetch(value, back, core):
        return shifted(value, axis, [(2 * (c - back) + 1, 2 * c + core) for c in range(back, chips)])

    far_last = unpack(fetch(packed, 7, 1), *shapes)
    far_next = unpack(fetch(packed, 5, 1), *shapes)
    near_last = unpack(fetch(packed, 3, 0), *shapes)
    near_next = unpack(fetch(packed, 1, 0), *shapes)
    near_next, ride = lax.optimization_barrier((near_next, ride))
    near = fold(near_last, near_next)
    far = fold(far_last, far_next)
    held = jnp.where(even, pack(*near), pack(*far))
    swap = [(2 * c, 2 * c + 1) for c in range(chips)] + [(2 * c + 1, 2 * c) for c in range(chips)]
    other = shifted(held, axis, swap)
    near_gain, near_state = unpack(jnp.where(even, held, other), *shapes)
    _, far_state = unpack(jnp.where(even, other, held), *shapes)
    behind = near_gain[..., None, None] * far_state + near_state
    odd_entering = pair[0][..., None, None] * behind + pair[1]
    return jnp.where(even, behind, odd_entering), ride


def summed_over(value, axis):
    count = lax.axis_size(axis)
    spread = jnp.broadcast_to(value[None], (count,) + value.shape)
    return lax.all_to_all(spread, axis, 0, 0, tiled=False).sum(0)


def causal_conv(window, window_ids, weight, bias, rows):
    taps = weight.shape[0]
    own_ids = window_ids[taps - 1 :]
    extra = (1,) * (window.ndim - 1)
    result = jnp.broadcast_to(bias, (rows,) + bias.shape)
    for offset in range(taps):
        piece = window[offset : offset + rows].astype(jnp.float32)
        same = (window_ids[offset : offset + rows] == own_ids).reshape((rows,) + extra)
        result = result + jnp.where(same, piece * weight[offset].astype(jnp.float32), 0.0)
    return jax.nn.silu(result).astype(jnp.bfloat16)


def on_device(
    x_proj,
    bc_proj,
    z_proj,
    dt_raw,
    conv_x,
    conv_bc,
    bias_x,
    bias_bc,
    dt_bias,
    a_log,
    d_skip,
    norm_gain,
    seg_ids,
):
    tok_rows, inner_local = x_proj.shape
    heads_local = dt_raw.shape[1]
    state_size = STATE
    groups_local = bc_proj.shape[2] // state_size
    heads_group = heads_local // groups_local
    head_size = inner_local // heads_local
    block = STRETCH
    blocks = tok_rows // block
    margin = conv_x.shape[0] - 1
    bc_width = bc_proj.shape[1] * bc_proj.shape[2]
    rim = jnp.concatenate(
        [
            x_proj[tok_rows - margin :],
            bc_proj[tok_rows - margin :].reshape(margin, bc_width),
            jnp.broadcast_to(seg_ids[tok_rows - margin :, None].astype(jnp.bfloat16), (margin, 128)),
        ],
        axis=1,
    )
    rim = from_behind(rim, "seq", 1)
    rim_x = rim[:, :inner_local]
    rim_bc = rim[:, inner_local : inner_local + bc_width].reshape(margin, *bc_proj.shape[1:])
    rim_ids = rim[:, inner_local + bc_width]
    own_ids = seg_ids.astype(jnp.float32)
    window_ids = jnp.concatenate([rim_ids.astype(jnp.float32), own_ids])
    x_conv = causal_conv(jnp.concatenate([rim_x, x_proj]), window_ids, conv_x, bias_x, tok_rows)
    bc_conv = causal_conv(
        jnp.concatenate([rim_bc, bc_proj]), window_ids, conv_bc, bias_bc, tok_rows
    )
    step_size = jax.nn.softplus(dt_raw + dt_bias)
    log_decay = step_size * -jnp.exp(a_log)
    cumul = jnp.cumsum(log_decay.reshape(blocks, block, heads_local), axis=1)
    cum_heads = cumul.reshape(blocks, block, groups_local, heads_group).transpose(0, 2, 3, 1)
    step_heads = step_size.reshape(blocks, block, groups_local, heads_group).transpose(0, 2, 3, 1)
    block_ids = own_ids.reshape(blocks, block)
    before_ids = window_ids[margin - 1 : margin - 1 + tok_rows : block]
    b_in = bc_conv[:, 0].reshape(blocks, block, groups_local, state_size)
    c_out = bc_conv[:, 1].reshape(blocks, block, groups_local, state_size)
    lower = jnp.tril(jnp.ones((block, block), dtype=bool))
    same = (block_ids[:, :, None] == block_ids[:, None, :]) & lower
    scores = jnp.einsum("cqgn,csgn->cgqs", c_out, b_in, preferred_element_type=jnp.float32)
    same_heads = same[:, None, None]
    spread = cum_heads[..., :, None] - cum_heads[..., None, :]
    decay = jnp.where(same_heads, jnp.exp(jnp.where(same_heads, spread, 0.0)), 0.0)
    mixing = (scores[:, :, None] * decay * step_heads[..., None, :]).astype(jnp.bfloat16)
    x_heads = x_conv.reshape(blocks, block, groups_local, heads_group, head_size)
    y_intra = jnp.einsum("cghqs,csghp->cqghp", mixing, x_heads, preferred_element_type=jnp.float32)
    tail_same = (block_ids == block_ids[:, -1:]).astype(jnp.float32)[:, None, None, :]
    weights = jnp.exp(cum_heads[..., -1:] - cum_heads) * step_heads * tail_same
    b_weighted = (
        b_in.transpose(0, 2, 1, 3)[:, :, None].astype(jnp.float32) * weights[..., None]
    ).astype(jnp.bfloat16)
    increment = jnp.einsum(
        "cghsn,csghp->cghpn", b_weighted, x_heads, preferred_element_type=jnp.float32
    )
    carry_gain = (
        jnp.exp(cum_heads[..., -1])
        * (block_ids[:, -1] == before_ids).astype(jnp.float32)[:, None, None]
    )
    link = (
        jnp.exp(cum_heads)
        * (block_ids == before_ids[:, None]).astype(jnp.float32)[:, None, None, :]
    )
    c_float = c_out.astype(jnp.float32)

    def recur(start_state):
        stacked = []
        current = start_state
        for index in range(blocks):
            stacked.append(current)
            current = carry_gain[index][..., None, None] * current + increment[index]
        return (jnp.stack(stacked), current)

    empty = jnp.zeros((groups_local, heads_group, head_size, state_size), jnp.float32)
    zero_states, summary = recur(empty)
    device_gain = carry_gain[0] * carry_gain[1]
    skip = d_skip.reshape(groups_local, heads_group)[..., None]
    base = y_intra + skip * x_heads.astype(jnp.float32)
    entering, base = entering_state(device_gain, summary, "seq", base)
    states, _ = recur(entering)
    product = jnp.einsum("cqgn,cghpn->cqghp", c_float, states, precision=lax.Precision.HIGHEST)
    y_inter = product * link.transpose(0, 3, 1, 2)[..., None]
    mixed = base + y_inter
    gated = mixed.reshape(tok_rows, inner_local) * jax.nn.silu(z_proj.astype(jnp.float32))
    squares = summed_over(jnp.sum(gated * gated, axis=-1), "tp")
    scale = lax.rsqrt(squares / (inner_local * lax.axis_size("tp")) + 1e-05)
    return (gated * scale[:, None] * norm_gain).astype(jnp.bfloat16)


def solution(mesh):
    in_specs = (
        P("seq", "tp"),
        P("seq", None, "tp"),
        P("seq", "tp"),
        P("seq", "tp"),
        P(None, "tp"),
        P(None, None, "tp"),
        P("tp"),
        P(None, "tp"),
        P("tp"),
        P("tp"),
        P("tp"),
        P("tp"),
        P("seq"),
    )
    out_specs = P("seq", "tp")
    return jax.shard_map(
        on_device, mesh=mesh, in_specs=in_specs, out_specs=out_specs, check_vma=False
    )
```

```python
import jax
import jax.numpy as jnp
from jax import lax
from jax.sharding import PartitionSpec as P

STATE = 128
STRETCH = 256


def from_behind(block, axis, distance):
    devices = range(lax.axis_size(axis))
    route = [(i - distance, i) for i in devices if i - distance in devices]
    return lax.ppermute(block, axis, route)


def shifted(block, axis, pairs):
    return lax.ppermute(block, axis, pairs)


def fold(earlier, later):
    gain_e, state_e = earlier
    gain_l, state_l = later
    return (gain_e * gain_l, gain_l[..., None, None] * state_e + state_l)


def pack(gain, state):
    lanes = state.shape[-1]
    flat = state.reshape(-1, lanes)
    row = jnp.zeros((8, lanes), state.dtype).at[0, : gain.size].set(gain.reshape(-1))
    return jnp.concatenate([flat, row])


def unpack(packed, gain_shape, state_shape):
    rows = packed.shape[0] - 8
    count = 1
    for size in gain_shape:
        count *= size
    return (packed[rows, :count].reshape(gain_shape), packed[:rows].reshape(state_shape))


def entering_state(gain, state, axis, ride):
    count = lax.axis_size(axis)
    chips = count // 2
    shapes = (gain.shape, state.shape)
    own = (gain, state)
    pair = unpack(shifted(pack(*own), axis, [(2 * c, 2 * c + 1) for c in range(chips)]), *shapes)
    chip_total = fold(pair, own)
    route = [(2 * c + 1, 2 * (c + 1) + 1) for c in range(chips - 1)]
    chip_total = fold(unpack(shifted(pack(*chip_total), axis, route), *shapes), chip_total)
    mine = lax.axis_index(axis)
    even = mine % 2 == 0
    packed = pack(*chip_total)

    def fetch(value, back, core):
        return shifted(value, axis, [(2 * (c - back) + 1, 2 * c + core) for c in range(back, chips)])

    far_last = unpack(fetch(packed, 7, 1), *shapes)
    far_next = unpack(fetch(packed, 5, 1), *shapes)
    near_last = unpack(fetch(packed, 3, 0), *shapes)
    near_next = unpack(fetch(packed, 1, 0), *shapes)
    near_next, ride = lax.optimization_barrier((near_next, ride))
    near = fold(near_last, near_next)
    far = fold(far_last, far_next)
    own = even.astype(jnp.float32)
    peer = 1.0 - own
    held = own * pack(*near) + peer * pack(*far)
    swap = [(2 * c, 2 * c + 1) for c in range(chips)] + [(2 * c + 1, 2 * c) for c in range(chips)]
    other = shifted(held, axis, swap)
    held_gain, held_state = unpack(held, *shapes)
    other_gain, other_state = unpack(other, *shapes)
    near_gain = own * held_gain + peer * other_gain
    near_state = own * held_state + peer * other_state
    far_state = own * other_state + peer * held_state
    behind = near_gain[..., None, None] * far_state + near_state
    odd_entering = pair[0][..., None, None] * behind + pair[1]
    return own * behind + peer * odd_entering, ride


def summed_over(value, axis):
    count = lax.axis_size(axis)
    spread = jnp.broadcast_to(value[None], (count,) + value.shape)
    return lax.all_to_all(spread, axis, 0, 0, tiled=False).sum(0)


def causal_conv(window, window_ids, weight, bias, rows):
    taps = weight.shape[0]
    own_ids = window_ids[taps - 1 :]
    extra = (1,) * (window.ndim - 1)
    result = jnp.broadcast_to(bias, (rows,) + bias.shape)
    for offset in range(taps):
        piece = window[offset : offset + rows].astype(jnp.float32)
        same = (window_ids[offset : offset + rows] == own_ids).reshape((rows,) + extra)
        result = result + jnp.where(same, piece * weight[offset].astype(jnp.float32), 0.0)
    return jax.nn.silu(result).astype(jnp.bfloat16)


def on_device(
    x_proj,
    bc_proj,
    z_proj,
    dt_raw,
    conv_x,
    conv_bc,
    bias_x,
    bias_bc,
    dt_bias,
    a_log,
    d_skip,
    norm_gain,
    seg_ids,
):
    tok_rows, inner_local = x_proj.shape
    heads_local = dt_raw.shape[1]
    state_size = STATE
    groups_local = bc_proj.shape[2] // state_size
    heads_group = heads_local // groups_local
    head_size = inner_local // heads_local
    block = STRETCH
    blocks = tok_rows // block
    margin = conv_x.shape[0] - 1
    bc_width = bc_proj.shape[1] * bc_proj.shape[2]
    rim = jnp.concatenate(
        [
            x_proj[tok_rows - margin :],
            bc_proj[tok_rows - margin :].reshape(margin, bc_width),
            jnp.broadcast_to(seg_ids[tok_rows - margin :, None].astype(jnp.bfloat16), (margin, 128)),
        ],
        axis=1,
    )
    rim = from_behind(rim, "seq", 1)
    rim_x = rim[:, :inner_local]
    rim_bc = rim[:, inner_local : inner_local + bc_width].reshape(margin, *bc_proj.shape[1:])
    rim_ids = rim[:, inner_local + bc_width]
    own_ids = seg_ids.astype(jnp.float32)
    window_ids = jnp.concatenate([rim_ids.astype(jnp.float32), own_ids])
    x_conv = causal_conv(jnp.concatenate([rim_x, x_proj]), window_ids, conv_x, bias_x, tok_rows)
    bc_conv = causal_conv(
        jnp.concatenate([rim_bc, bc_proj]), window_ids, conv_bc, bias_bc, tok_rows
    )
    step_size = jax.nn.softplus(dt_raw + dt_bias)
    log_decay = step_size * -jnp.exp(a_log)
    cumul = jnp.cumsum(log_decay.reshape(blocks, block, heads_local), axis=1)
    cum_heads = cumul.reshape(blocks, block, groups_local, heads_group).transpose(0, 2, 3, 1)
    step_heads = step_size.reshape(blocks, block, groups_local, heads_group).transpose(0, 2, 3, 1)
    block_ids = own_ids.reshape(blocks, block)
    before_ids = window_ids[margin - 1 : margin - 1 + tok_rows : block]
    b_in = bc_conv[:, 0].reshape(blocks, block, groups_local, state_size)
    c_out = bc_conv[:, 1].reshape(blocks, block, groups_local, state_size)
    lower = jnp.tril(jnp.ones((block, block), dtype=bool))
    same = (block_ids[:, :, None] == block_ids[:, None, :]) & lower
    scores = jnp.einsum("cqgn,csgn->cgqs", c_out, b_in, preferred_element_type=jnp.float32)
    same_heads = same[:, None, None]
    spread = cum_heads[..., :, None] - cum_heads[..., None, :]
    decay = jnp.where(same_heads, jnp.exp(jnp.where(same_heads, spread, 0.0)), 0.0)
    mixing = (scores[:, :, None] * decay * step_heads[..., None, :]).astype(jnp.bfloat16)
    x_heads = x_conv.reshape(blocks, block, groups_local, heads_group, head_size)
    y_intra = jnp.einsum("cghqs,csghp->cqghp", mixing, x_heads, preferred_element_type=jnp.float32)
    tail_same = (block_ids == block_ids[:, -1:]).astype(jnp.float32)[:, None, None, :]
    weights = jnp.exp(cum_heads[..., -1:] - cum_heads) * step_heads * tail_same
    b_weighted = (
        b_in.transpose(0, 2, 1, 3)[:, :, None].astype(jnp.float32) * weights[..., None]
    ).astype(jnp.bfloat16)
    increment = jnp.einsum(
        "cghsn,csghp->cghpn", b_weighted, x_heads, preferred_element_type=jnp.float32
    )
    carry_gain = (
        jnp.exp(cum_heads[..., -1])
        * (block_ids[:, -1] == before_ids).astype(jnp.float32)[:, None, None]
    )
    link = (
        jnp.exp(cum_heads)
        * (block_ids == before_ids[:, None]).astype(jnp.float32)[:, None, None, :]
    )
    c_float = c_out.astype(jnp.float32)

    def recur(start_state):
        stacked = []
        current = start_state
        for index in range(blocks):
            stacked.append(current)
            current = carry_gain[index][..., None, None] * current + increment[index]
        return (jnp.stack(stacked), current)

    empty = jnp.zeros((groups_local, heads_group, head_size, state_size), jnp.float32)
    zero_states, summary = recur(empty)
    device_gain = carry_gain[0] * carry_gain[1]
    skip = d_skip.reshape(groups_local, heads_group)[..., None]
    base = y_intra + skip * x_heads.astype(jnp.float32)
    entering, base = entering_state(device_gain, summary, "seq", base)
    states, _ = recur(entering)
    product = jnp.einsum("cqgn,cghpn->cqghp", c_float, states, precision=lax.Precision.HIGHEST)
    y_inter = product * link.transpose(0, 3, 1, 2)[..., None]
    mixed = base + y_inter
    gated = mixed.reshape(tok_rows, inner_local) * jax.nn.silu(z_proj.astype(jnp.float32))
    squares = summed_over(jnp.sum(gated * gated, axis=-1), "tp")
    scale = lax.rsqrt(squares / (inner_local * lax.axis_size("tp")) + 1e-05)
    return (gated * scale[:, None] * norm_gain).astype(jnp.bfloat16)


def solution(mesh):
    in_specs = (
        P("seq", "tp"),
        P("seq", None, "tp"),
        P("seq", "tp"),
        P("seq", "tp"),
        P(None, "tp"),
        P(None, None, "tp"),
        P("tp"),
        P(None, "tp"),
        P("tp"),
        P("tp"),
        P("tp"),
        P("tp"),
        P("seq"),
    )
    out_specs = P("seq", "tp")
    return jax.shard_map(
        on_device, mesh=mesh, in_specs=in_specs, out_specs=out_specs, check_vma=False
    )
```

```python
import jax
import jax.numpy as jnp
from jax import lax
from jax.sharding import PartitionSpec as P

STATE = 128
STRETCH = 256


def from_behind(block, axis, distance):
    devices = range(lax.axis_size(axis))
    route = [(i - distance, i) for i in devices if i - distance in devices]
    return lax.ppermute(block, axis, route)


def shifted(block, axis, pairs):
    return lax.ppermute(block, axis, pairs)


def fold(earlier, later):
    gain_e, state_e = earlier
    gain_l, state_l = later
    return (gain_e * gain_l, gain_l[..., None, None] * state_e + state_l)


def pack(gain, state):
    lanes = state.shape[-1]
    flat = state.reshape(-1, lanes)
    row = jnp.zeros((8, lanes), state.dtype).at[0, : gain.size].set(gain.reshape(-1))
    return jnp.concatenate([flat, row])


def unpack(packed, gain_shape, state_shape):
    rows = packed.shape[0] - 8
    count = 1
    for size in gain_shape:
        count *= size
    return (packed[rows, :count].reshape(gain_shape), packed[:rows].reshape(state_shape))


def entering_state(gain, state, axis, ride):
    count = lax.axis_size(axis)
    chips = count // 2
    shapes = (gain.shape, state.shape)
    own = (gain, state)
    pair = unpack(shifted(pack(*own), axis, [(2 * c, 2 * c + 1) for c in range(chips)]), *shapes)
    chip_total = fold(pair, own)
    route = [(2 * c + 1, 2 * (c + 1) + 1) for c in range(chips - 1)]
    chip_total = fold(unpack(shifted(pack(*chip_total), axis, route), *shapes), chip_total)
    mine = lax.axis_index(axis)
    even = mine % 2 == 0
    packed = pack(*chip_total)

    def fetch(value, back, core):
        return shifted(value, axis, [(2 * (c - back) + 1, 2 * c + core) for c in range(back, chips)])

    far_last = unpack(fetch(packed, 7, 1), *shapes)
    far_next = unpack(fetch(packed, 5, 1), *shapes)
    near_last = unpack(fetch(packed, 3, 0), *shapes)
    near_next = unpack(fetch(packed, 1, 0), *shapes)
    near_next, ride = lax.optimization_barrier((near_next, ride))
    near = fold(near_last, near_next)
    far = fold(far_last, far_next)
    held = jnp.where(even, pack(*near), pack(*far))
    swap = [(2 * c, 2 * c + 1) for c in range(chips)] + [(2 * c + 1, 2 * c) for c in range(chips)]
    other = shifted(held, axis, swap)
    near_gain, near_state = unpack(jnp.where(even, held, other), *shapes)
    _, far_state = unpack(jnp.where(even, other, held), *shapes)
    behind = near_gain[..., None, None] * far_state + near_state
    odd_entering = pair[0][..., None, None] * behind + pair[1]
    return jnp.where(even, behind, odd_entering), ride


def summed_over(value, axis):
    count = lax.axis_size(axis)
    spread = jnp.broadcast_to(value[None], (count,) + value.shape)
    return lax.all_to_all(spread, axis, 0, 0, tiled=False).sum(0)


def causal_conv(window, window_ids, weight, bias, rows):
    taps = weight.shape[0]
    own_ids = window_ids[taps - 1 :]
    extra = (1,) * (window.ndim - 1)
    result = jnp.broadcast_to(bias, (rows,) + bias.shape)
    for offset in range(taps):
        piece = window[offset : offset + rows].astype(jnp.float32)
        same = (window_ids[offset : offset + rows] == own_ids).reshape((rows,) + extra)
        result = result + jnp.where(same, piece * weight[offset].astype(jnp.float32), 0.0)
    return jax.nn.silu(result).astype(jnp.bfloat16)


def on_device(
    x_proj,
    bc_proj,
    z_proj,
    dt_raw,
    conv_x,
    conv_bc,
    bias_x,
    bias_bc,
    dt_bias,
    a_log,
    d_skip,
    norm_gain,
    seg_ids,
):
    tok_rows, inner_local = x_proj.shape
    heads_local = dt_raw.shape[1]
    state_size = STATE
    groups_local = bc_proj.shape[2] // state_size
    heads_group = heads_local // groups_local
    head_size = inner_local // heads_local
    block = STRETCH
    blocks = tok_rows // block
    margin = conv_x.shape[0] - 1
    bc_width = bc_proj.shape[1] * bc_proj.shape[2]
    rim = jnp.concatenate(
        [
            x_proj[tok_rows - margin :],
            bc_proj[tok_rows - margin :].reshape(margin, bc_width),
            jnp.broadcast_to(seg_ids[tok_rows - margin :, None].astype(jnp.bfloat16), (margin, 128)),
        ],
        axis=1,
    )
    rim = from_behind(rim, "seq", 1)
    rim_x = rim[:, :inner_local]
    rim_bc = rim[:, inner_local : inner_local + bc_width].reshape(margin, *bc_proj.shape[1:])
    rim_ids = rim[:, inner_local + bc_width]
    own_ids = seg_ids.astype(jnp.float32)
    window_ids = jnp.concatenate([rim_ids.astype(jnp.float32), own_ids])
    x_conv = causal_conv(jnp.concatenate([rim_x, x_proj]), window_ids, conv_x, bias_x, tok_rows)
    bc_conv = causal_conv(
        jnp.concatenate([rim_bc, bc_proj]), window_ids, conv_bc, bias_bc, tok_rows
    )
    step_size = jax.nn.softplus(dt_raw + dt_bias)
    log_decay = step_size * -jnp.exp(a_log)
    cumul = jnp.cumsum(log_decay.reshape(blocks, block, heads_local), axis=1)
    cum_heads = cumul.reshape(blocks, block, groups_local, heads_group).transpose(0, 2, 3, 1)
    step_heads = step_size.reshape(blocks, block, groups_local, heads_group).transpose(0, 2, 3, 1)
    block_ids = own_ids.reshape(blocks, block)
    before_ids = window_ids[margin - 1 : margin - 1 + tok_rows : block]
    b_in = bc_conv[:, 0].reshape(blocks, block, groups_local, state_size)
    c_out = bc_conv[:, 1].reshape(blocks, block, groups_local, state_size)
    lower = jnp.tril(jnp.ones((block, block), dtype=bool))
    same = (block_ids[:, :, None] == block_ids[:, None, :]) & lower
    scores = jnp.einsum("cqgn,csgn->cgqs", c_out, b_in, preferred_element_type=jnp.float32)
    same_heads = same[:, None, None]
    spread = cum_heads[..., :, None] - cum_heads[..., None, :]
    decay = jnp.where(same_heads, jnp.exp(jnp.where(same_heads, spread, 0.0)), 0.0)
    mixing = (scores[:, :, None] * decay * step_heads[..., None, :]).astype(jnp.bfloat16)
    x_heads = x_conv.reshape(blocks, block, groups_local, heads_group, head_size)
    y_intra = jnp.einsum("cghqs,csghp->cqghp", mixing, x_heads, preferred_element_type=jnp.float32)
    tail_same = (block_ids == block_ids[:, -1:]).astype(jnp.float32)[:, None, None, :]
    weights = jnp.exp(cum_heads[..., -1:] - cum_heads) * step_heads * tail_same
    b_weighted = (
        b_in.transpose(0, 2, 1, 3)[:, :, None].astype(jnp.float32) * weights[..., None]
    ).astype(jnp.bfloat16)
    increment = jnp.einsum(
        "cghsn,csghp->cghpn", b_weighted, x_heads, preferred_element_type=jnp.float32
    )
    carry_gain = (
        jnp.exp(cum_heads[..., -1])
        * (block_ids[:, -1] == before_ids).astype(jnp.float32)[:, None, None]
    )
    link = (
        jnp.exp(cum_heads)
        * (block_ids == before_ids[:, None]).astype(jnp.float32)[:, None, None, :]
    )
    c_float = c_out.astype(jnp.float32)

    def recur(start_state):
        stacked = []
        current = start_state
        for index in range(blocks):
            stacked.append(current)
            current = carry_gain[index][..., None, None] * current + increment[index]
        return (jnp.stack(stacked), current)

    empty = jnp.zeros((groups_local, heads_group, head_size, state_size), jnp.float32)
    zero_states, summary = recur(empty)
    device_gain = carry_gain[0] * carry_gain[1]
    skip = d_skip.reshape(groups_local, heads_group)[..., None]
    base = y_intra + skip * x_heads.astype(jnp.float32)
    entering, base = entering_state(device_gain, summary, "seq", base)
    states, _ = recur(entering)
    product = jnp.einsum("cqgn,cghpn->cqghp", c_float, states, precision=lax.Precision.HIGHEST)
    y_inter = product * link.transpose(0, 3, 1, 2)[..., None]
    mixed = base + y_inter
    gate = jax.nn.silu(z_proj.astype(jnp.float32)).reshape(mixed.shape)
    gated = mixed * gate
    squares = summed_over(jnp.sum(gated * gated, axis=(2, 3, 4)).reshape(tok_rows), "tp")
    gated = gated.reshape(tok_rows, inner_local)
    scale = lax.rsqrt(squares / (inner_local * lax.axis_size("tp")) + 1e-05)
    return (gated * scale[:, None] * norm_gain).astype(jnp.bfloat16)


def solution(mesh):
    in_specs = (
        P("seq", "tp"),
        P("seq", None, "tp"),
        P("seq", "tp"),
        P("seq", "tp"),
        P(None, "tp"),
        P(None, None, "tp"),
        P("tp"),
        P(None, "tp"),
        P("tp"),
        P("tp"),
        P("tp"),
        P("tp"),
        P("seq"),
    )
    out_specs = P("seq", "tp")
    return jax.shard_map(
        on_device, mesh=mesh, in_specs=in_specs, out_specs=out_specs, check_vma=False
    )
```

```python
import jax
import jax.numpy as jnp
from jax import lax
from jax.sharding import PartitionSpec as P

STATE = 128
STRETCH = 256


def from_behind(block, axis, distance):
    devices = range(lax.axis_size(axis))
    route = [(i - distance, i) for i in devices if i - distance in devices]
    return lax.ppermute(block, axis, route)


def shifted(block, axis, pairs):
    return lax.ppermute(block, axis, pairs)


def fold(earlier, later):
    gain_e, state_e = earlier
    gain_l, state_l = later
    return (gain_e * gain_l, gain_l[..., None, None] * state_e + state_l)


def pack(gain, state):
    lanes = state.shape[-1]
    flat = state.reshape(-1, lanes)
    row = jnp.zeros((8, lanes), state.dtype).at[0, : gain.size].set(gain.reshape(-1))
    return jnp.concatenate([flat, row])


def unpack(packed, gain_shape, state_shape):
    rows = packed.shape[0] - 8
    count = 1
    for size in gain_shape:
        count *= size
    return (packed[rows, :count].reshape(gain_shape), packed[:rows].reshape(state_shape))


def entering_state(gain, state, axis, ride):
    count = lax.axis_size(axis)
    chips = count // 2
    shapes = (gain.shape, state.shape)
    own = (gain, state)
    pair = unpack(shifted(pack(*own), axis, [(2 * c, 2 * c + 1) for c in range(chips)]), *shapes)
    chip_total = fold(pair, own)
    route = [(2 * c + 1, 2 * (c + 1) + 1) for c in range(chips - 1)]
    chip_total = fold(unpack(shifted(pack(*chip_total), axis, route), *shapes), chip_total)
    mine = lax.axis_index(axis)
    even = mine % 2 == 0
    packed = pack(*chip_total)

    def fetch(value, back, core):
        return shifted(value, axis, [(2 * (c - back) + 1, 2 * c + core) for c in range(back, chips)])

    far_last = unpack(fetch(packed, 7, 1), *shapes)
    far_next = unpack(fetch(packed, 5, 1), *shapes)
    near_last = unpack(fetch(packed, 3, 0), *shapes)
    near_next = unpack(fetch(packed, 1, 0), *shapes)
    near_next, ride = lax.optimization_barrier((near_next, ride))
    near = fold(near_last, near_next)
    far = fold(far_last, far_next)
    held = jnp.where(even, pack(*near), pack(*far))
    swap = [(2 * c, 2 * c + 1) for c in range(chips)] + [(2 * c + 1, 2 * c) for c in range(chips)]
    other = shifted(held, axis, swap)
    near_gain, near_state = unpack(jnp.where(even, held, other), *shapes)
    _, far_state = unpack(jnp.where(even, other, held), *shapes)
    behind = near_gain[..., None, None] * far_state + near_state
    odd_entering = pair[0][..., None, None] * behind + pair[1]
    return jnp.where(even, behind, odd_entering), ride


def summed_over(value, axis):
    count = lax.axis_size(axis)
    spread = jnp.broadcast_to(value[None], (count,) + value.shape)
    return lax.all_to_all(spread, axis, 0, 0, tiled=False).sum(0)


def causal_conv(window, window_ids, weight, bias, rows):
    taps = weight.shape[0]
    own_ids = window_ids[taps - 1 :]
    extra = (1,) * (window.ndim - 1)
    result = jnp.broadcast_to(bias, (rows,) + bias.shape)
    for offset in range(taps):
        piece = window[offset : offset + rows].astype(jnp.float32)
        same = (window_ids[offset : offset + rows] == own_ids).reshape((rows,) + extra)
        result = result + jnp.where(same, piece * weight[offset].astype(jnp.float32), 0.0)
    return jax.nn.silu(result).astype(jnp.bfloat16)


def on_device(
    x_proj,
    bc_proj,
    z_proj,
    dt_raw,
    conv_x,
    conv_bc,
    bias_x,
    bias_bc,
    dt_bias,
    a_log,
    d_skip,
    norm_gain,
    seg_ids,
):
    tok_rows, inner_local = x_proj.shape
    heads_local = dt_raw.shape[1]
    state_size = STATE
    groups_local = bc_proj.shape[2] // state_size
    heads_group = heads_local // groups_local
    head_size = inner_local // heads_local
    block = STRETCH
    blocks = tok_rows // block
    margin = conv_x.shape[0] - 1
    bc_width = bc_proj.shape[1] * bc_proj.shape[2]
    rim = jnp.concatenate(
        [
            x_proj[tok_rows - margin :],
            bc_proj[tok_rows - margin :].reshape(margin, bc_width),
            jnp.broadcast_to(seg_ids[tok_rows - margin :, None].astype(jnp.bfloat16), (margin, 128)),
        ],
        axis=1,
    )
    rim = from_behind(rim, "seq", 1)
    rim_x = rim[:, :inner_local]
    rim_bc = rim[:, inner_local : inner_local + bc_width].reshape(margin, *bc_proj.shape[1:])
    rim_ids = rim[:, inner_local + bc_width]
    own_ids = seg_ids.astype(jnp.float32)
    window_ids = jnp.concatenate([rim_ids.astype(jnp.float32), own_ids])
    x_conv = causal_conv(jnp.concatenate([rim_x, x_proj]), window_ids, conv_x, bias_x, tok_rows)
    bc_conv = causal_conv(
        jnp.concatenate([rim_bc, bc_proj]), window_ids, conv_bc, bias_bc, tok_rows
    )
    step_size = jax.nn.softplus(dt_raw + dt_bias)
    log_decay = step_size * -jnp.exp(a_log)
    cumul = jnp.cumsum(log_decay.reshape(blocks, block, heads_local), axis=1)
    cum_heads = cumul.reshape(blocks, block, groups_local, heads_group).transpose(0, 2, 3, 1)
    step_heads = step_size.reshape(blocks, block, groups_local, heads_group).transpose(0, 2, 3, 1)
    block_ids = own_ids.reshape(blocks, block)
    before_ids = window_ids[margin - 1 : margin - 1 + tok_rows : block]
    b_in = bc_conv[:, 0].reshape(blocks, block, groups_local, state_size)
    c_out = bc_conv[:, 1].reshape(blocks, block, groups_local, state_size)
    lower = jnp.tril(jnp.ones((block, block), dtype=bool))
    same = (block_ids[:, :, None] == block_ids[:, None, :]) & lower
    scores = jnp.einsum("cqgn,csgn->cgqs", c_out, b_in, preferred_element_type=jnp.float32)
    same_heads = same[:, None, None]
    spread = cum_heads[..., :, None] - cum_heads[..., None, :]
    decay = jnp.where(same_heads, jnp.exp(jnp.where(same_heads, spread, 0.0)), 0.0)
    mixing = (scores[:, :, None] * decay * step_heads[..., None, :]).astype(jnp.bfloat16)
    x_heads = x_conv.reshape(blocks, block, groups_local, heads_group, head_size)
    y_intra = jnp.einsum("cghqs,csghp->cqghp", mixing, x_heads, preferred_element_type=jnp.float32)
    tail_same = (block_ids == block_ids[:, -1:]).astype(jnp.float32)[:, None, None, :]
    weights = jnp.exp(cum_heads[..., -1:] - cum_heads) * step_heads * tail_same
    b_weighted = (
        b_in.transpose(0, 2, 1, 3)[:, :, None].astype(jnp.float32) * weights[..., None]
    ).astype(jnp.bfloat16)
    increment = jnp.einsum(
        "cghsn,csghp->cghpn", b_weighted, x_heads, preferred_element_type=jnp.float32
    )
    carry_gain = (
        jnp.exp(cum_heads[..., -1])
        * (block_ids[:, -1] == before_ids).astype(jnp.float32)[:, None, None]
    )
    link = (
        jnp.exp(cum_heads)
        * (block_ids == before_ids[:, None]).astype(jnp.float32)[:, None, None, :]
    )
    c_float = c_out.astype(jnp.float32)

    def recur(start_state):
        stacked = []
        current = start_state
        for index in range(blocks):
            stacked.append(current)
            current = carry_gain[index][..., None, None] * current + increment[index]
        return (jnp.stack(stacked), current)

    empty = jnp.zeros((groups_local, heads_group, head_size, state_size), jnp.float32)
    zero_states, summary = recur(empty)
    device_gain = carry_gain[0] * carry_gain[1]
    skip = d_skip.reshape(groups_local, heads_group)[..., None]
    base = y_intra + skip * x_heads.astype(jnp.float32)
    entering, base = entering_state(device_gain, summary, "seq", base)
    states, _ = recur(entering)
    high = states.astype(jnp.bfloat16)
    rest = (states - high.astype(jnp.float32)).astype(jnp.bfloat16)
    product = jnp.einsum("cqgn,cghpn->cqghp", c_out, high, preferred_element_type=jnp.float32)
    product = product + jnp.einsum("cqgn,cghpn->cqghp", c_out, rest, preferred_element_type=jnp.float32)
    y_inter = product * link.transpose(0, 3, 1, 2)[..., None]
    mixed = base + y_inter
    gated = mixed.reshape(tok_rows, inner_local) * jax.nn.silu(z_proj.astype(jnp.float32))
    squares = summed_over(jnp.sum(gated * gated, axis=-1), "tp")
    scale = lax.rsqrt(squares / (inner_local * lax.axis_size("tp")) + 1e-05)
    return (gated * scale[:, None] * norm_gain).astype(jnp.bfloat16)


def solution(mesh):
    in_specs = (
        P("seq", "tp"),
        P("seq", None, "tp"),
        P("seq", "tp"),
        P("seq", "tp"),
        P(None, "tp"),
        P(None, None, "tp"),
        P("tp"),
        P(None, "tp"),
        P("tp"),
        P("tp"),
        P("tp"),
        P("tp"),
        P("seq"),
    )
    out_specs = P("seq", "tp")
    return jax.shard_map(
        on_device, mesh=mesh, in_specs=in_specs, out_specs=out_specs, check_vma=False
    )
```

```python
import jax
import jax.numpy as jnp
from jax import lax
from jax.sharding import PartitionSpec as P
from jax.experimental import pallas as pl

STATE = 128
STRETCH = 256


def from_behind(block, axis, distance):
    devices = range(lax.axis_size(axis))
    route = [(i - distance, i) for i in devices if i - distance in devices]
    return lax.ppermute(block, axis, route)


def shifted(block, axis, pairs):
    return lax.ppermute(block, axis, pairs)


def fold(earlier, later):
    gain_e, state_e = earlier
    gain_l, state_l = later
    return (gain_e * gain_l, gain_l[..., None, None] * state_e + state_l)


def pack(gain, state):
    lanes = state.shape[-1]
    flat = state.reshape(-1, lanes)
    row = jnp.zeros((8, lanes), state.dtype).at[0, : gain.size].set(gain.reshape(-1))
    return jnp.concatenate([flat, row])


def unpack(packed, gain_shape, state_shape):
    rows = packed.shape[0] - 8
    count = 1
    for size in gain_shape:
        count *= size
    return (packed[rows, :count].reshape(gain_shape), packed[:rows].reshape(state_shape))


def entering_state(gain, state, axis, ride):
    count = lax.axis_size(axis)
    chips = count // 2
    shapes = (gain.shape, state.shape)
    own = (gain, state)
    pair = unpack(shifted(pack(*own), axis, [(2 * c, 2 * c + 1) for c in range(chips)]), *shapes)
    chip_total = fold(pair, own)
    route = [(2 * c + 1, 2 * (c + 1) + 1) for c in range(chips - 1)]
    chip_total = fold(unpack(shifted(pack(*chip_total), axis, route), *shapes), chip_total)
    mine = lax.axis_index(axis)
    even = mine % 2 == 0
    packed = pack(*chip_total)

    def fetch(value, back, core):
        return shifted(value, axis, [(2 * (c - back) + 1, 2 * c + core) for c in range(back, chips)])

    far_last = unpack(fetch(packed, 7, 1), *shapes)
    far_next = unpack(fetch(packed, 5, 1), *shapes)
    near_last = unpack(fetch(packed, 3, 0), *shapes)
    near_next = unpack(fetch(packed, 1, 0), *shapes)
    near_next, ride = lax.optimization_barrier((near_next, ride))
    near = fold(near_last, near_next)
    far = fold(far_last, far_next)
    held = jnp.where(even, pack(*near), pack(*far))
    swap = [(2 * c, 2 * c + 1) for c in range(chips)] + [(2 * c + 1, 2 * c) for c in range(chips)]
    other = shifted(held, axis, swap)
    near_gain, near_state = unpack(jnp.where(even, held, other), *shapes)
    _, far_state = unpack(jnp.where(even, other, held), *shapes)
    behind = near_gain[..., None, None] * far_state + near_state
    odd_entering = pair[0][..., None, None] * behind + pair[1]
    return jnp.where(even, behind, odd_entering), ride


def summed_over(value, axis):
    count = lax.axis_size(axis)
    spread = jnp.broadcast_to(value[None], (count,) + value.shape)
    return lax.all_to_all(spread, axis, 0, 0, tiled=False).sum(0)


def scale_kernel(g_ref, s_ref, w_ref, o_ref):
    o_ref[...] = (g_ref[...] * s_ref[...] * w_ref[...]).T.astype(o_ref.dtype)


def scaled_out(gated, scale, gain, block):
    rows, width = gated.shape
    return pl.pallas_call(
        scale_kernel,
        grid=(rows // block,),
        in_specs=[
            pl.BlockSpec((width, block), lambda i: (0, i)),
            pl.BlockSpec((1, block), lambda i: (0, i)),
            pl.BlockSpec((width, 1), lambda i: (0, 0)),
        ],
        out_specs=pl.BlockSpec((block, width), lambda i: (i, 0)),
        out_shape=jax.ShapeDtypeStruct((rows, width), jnp.bfloat16),
        cost_estimate=pl.CostEstimate(
            flops=2 * rows * width, transcendentals=0, bytes_accessed=6 * rows * width
        ),
    )(gated.T, scale[None, :], gain[:, None])


def causal_conv(window, window_ids, weight, bias, rows):
    taps = weight.shape[0]
    own_ids = window_ids[taps - 1 :]
    extra = (1,) * (window.ndim - 1)
    result = jnp.broadcast_to(bias, (rows,) + bias.shape)
    for offset in range(taps):
        piece = window[offset : offset + rows].astype(jnp.float32)
        same = (window_ids[offset : offset + rows] == own_ids).reshape((rows,) + extra)
        result = result + jnp.where(same, piece * weight[offset].astype(jnp.float32), 0.0)
    return jax.nn.silu(result).astype(jnp.bfloat16)


def on_device(
    x_proj,
    bc_proj,
    z_proj,
    dt_raw,
    conv_x,
    conv_bc,
    bias_x,
    bias_bc,
    dt_bias,
    a_log,
    d_skip,
    norm_gain,
    seg_ids,
):
    tok_rows, inner_local = x_proj.shape
    heads_local = dt_raw.shape[1]
    state_size = STATE
    groups_local = bc_proj.shape[2] // state_size
    heads_group = heads_local // groups_local
    head_size = inner_local // heads_local
    block = STRETCH
    blocks = tok_rows // block
    margin = conv_x.shape[0] - 1
    bc_width = bc_proj.shape[1] * bc_proj.shape[2]
    rim = jnp.concatenate(
        [
            x_proj[tok_rows - margin :],
            bc_proj[tok_rows - margin :].reshape(margin, bc_width),
            jnp.broadcast_to(seg_ids[tok_rows - margin :, None].astype(jnp.bfloat16), (margin, 128)),
        ],
        axis=1,
    )
    rim = from_behind(rim, "seq", 1)
    rim_x = rim[:, :inner_local]
    rim_bc = rim[:, inner_local : inner_local + bc_width].reshape(margin, *bc_proj.shape[1:])
    rim_ids = rim[:, inner_local + bc_width]
    own_ids = seg_ids.astype(jnp.float32)
    window_ids = jnp.concatenate([rim_ids.astype(jnp.float32), own_ids])
    x_conv = causal_conv(jnp.concatenate([rim_x, x_proj]), window_ids, conv_x, bias_x, tok_rows)
    bc_conv = causal_conv(
        jnp.concatenate([rim_bc, bc_proj]), window_ids, conv_bc, bias_bc, tok_rows
    )
    step_size = jax.nn.softplus(dt_raw + dt_bias)
    log_decay = step_size * -jnp.exp(a_log)
    cumul = jnp.cumsum(log_decay.reshape(blocks, block, heads_local), axis=1)
    cum_heads = cumul.reshape(blocks, block, groups_local, heads_group).transpose(0, 2, 3, 1)
    step_heads = step_size.reshape(blocks, block, groups_local, heads_group).transpose(0, 2, 3, 1)
    block_ids = own_ids.reshape(blocks, block)
    before_ids = window_ids[margin - 1 : margin - 1 + tok_rows : block]
    b_in = bc_conv[:, 0].reshape(blocks, block, groups_local, state_size)
    c_out = bc_conv[:, 1].reshape(blocks, block, groups_local, state_size)
    lower = jnp.tril(jnp.ones((block, block), dtype=bool))
    same = (block_ids[:, :, None] == block_ids[:, None, :]) & lower
    scores = jnp.einsum("cqgn,csgn->cgqs", c_out, b_in, preferred_element_type=jnp.float32)
    same_heads = same[:, None, None]
    spread = cum_heads[..., :, None] - cum_heads[..., None, :]
    decay = jnp.where(same_heads, jnp.exp(jnp.where(same_heads, spread, 0.0)), 0.0)
    mixing = (scores[:, :, None] * decay * step_heads[..., None, :]).astype(jnp.bfloat16)
    x_heads = x_conv.reshape(blocks, block, groups_local, heads_group, head_size)
    y_intra = jnp.einsum("cghqs,csghp->cqghp", mixing, x_heads, preferred_element_type=jnp.float32)
    tail_same = (block_ids == block_ids[:, -1:]).astype(jnp.float32)[:, None, None, :]
    weights = jnp.exp(cum_heads[..., -1:] - cum_heads) * step_heads * tail_same
    b_weighted = (
        b_in.transpose(0, 2, 1, 3)[:, :, None].astype(jnp.float32) * weights[..., None]
    ).astype(jnp.bfloat16)
    increment = jnp.einsum(
        "cghsn,csghp->cghpn", b_weighted, x_heads, preferred_element_type=jnp.float32
    )
    carry_gain = (
        jnp.exp(cum_heads[..., -1])
        * (block_ids[:, -1] == before_ids).astype(jnp.float32)[:, None, None]
    )
    link = (
        jnp.exp(cum_heads)
        * (block_ids == before_ids[:, None]).astype(jnp.float32)[:, None, None, :]
    )
    c_float = c_out.astype(jnp.float32)

    def recur(start_state):
        stacked = []
        current = start_state
        for index in range(blocks):
            stacked.append(current)
            current = carry_gain[index][..., None, None] * current + increment[index]
        return (jnp.stack(stacked), current)

    empty = jnp.zeros((groups_local, heads_group, head_size, state_size), jnp.float32)
    zero_states, summary = recur(empty)
    device_gain = carry_gain[0] * carry_gain[1]
    skip = d_skip.reshape(groups_local, heads_group)[..., None]
    base = y_intra + skip * x_heads.astype(jnp.float32)
    entering, base = entering_state(device_gain, summary, "seq", base)
    states, _ = recur(entering)
    product = jnp.einsum("cqgn,cghpn->cqghp", c_float, states, precision=lax.Precision.HIGHEST)
    y_inter = product * link.transpose(0, 3, 1, 2)[..., None]
    mixed = base + y_inter
    gated = mixed.reshape(tok_rows, inner_local) * jax.nn.silu(z_proj.astype(jnp.float32))
    squares = summed_over(jnp.sum(gated * gated, axis=-1), "tp")
    scale = lax.rsqrt(squares / (inner_local * lax.axis_size("tp")) + 1e-05)
    return scaled_out(gated, scale, norm_gain, block)


def solution(mesh):
    in_specs = (
        P("seq", "tp"),
        P("seq", None, "tp"),
        P("seq", "tp"),
        P("seq", "tp"),
        P(None, "tp"),
        P(None, None, "tp"),
        P("tp"),
        P(None, "tp"),
        P("tp"),
        P("tp"),
        P("tp"),
        P("tp"),
        P("seq"),
    )
    out_specs = P("seq", "tp")
    return jax.shard_map(
        on_device, mesh=mesh, in_specs=in_specs, out_specs=out_specs, check_vma=False
    )
```

```python
import jax
import jax.numpy as jnp
from jax import lax
from jax.sharding import PartitionSpec as P

STATE = 128
STRETCH = 256


def from_behind(block, axis, distance):
    devices = range(lax.axis_size(axis))
    route = [(i - distance, i) for i in devices if i - distance in devices]
    return lax.ppermute(block, axis, route)


def shifted(block, axis, pairs):
    return lax.ppermute(block, axis, pairs)


def fold(earlier, later):
    gain_e, state_e = earlier
    gain_l, state_l = later
    return (gain_e * gain_l, gain_l[..., None, None] * state_e + state_l)


def pack(gain, state):
    lanes = state.shape[-1]
    flat = state.reshape(-1, lanes)
    row = jnp.zeros((8, lanes), state.dtype).at[0, : gain.size].set(gain.reshape(-1))
    return jnp.concatenate([flat, row])


def unpack(packed, gain_shape, state_shape):
    rows = packed.shape[0] - 8
    count = 1
    for size in gain_shape:
        count *= size
    return (packed[rows, :count].reshape(gain_shape), packed[:rows].reshape(state_shape))


def entering_state(gain, state, axis, ride):
    count = lax.axis_size(axis)
    chips = count // 2
    shapes = (gain.shape, state.shape)
    own = (gain, state)
    pair = unpack(shifted(pack(*own), axis, [(2 * c, 2 * c + 1) for c in range(chips)]), *shapes)
    chip_total = fold(pair, own)
    route = [(2 * c + 1, 2 * (c + 1) + 1) for c in range(chips - 1)]
    chip_total = fold(unpack(shifted(pack(*chip_total), axis, route), *shapes), chip_total)
    mine = lax.axis_index(axis)
    even = mine % 2 == 0
    packed = pack(*chip_total)

    def fetch(value, back, core):
        return shifted(value, axis, [(2 * (c - back) + 1, 2 * c + core) for c in range(back, chips)])

    far_last = unpack(fetch(packed, 7, 1), *shapes)
    far_next = unpack(fetch(packed, 5, 1), *shapes)
    near_last = unpack(fetch(packed, 3, 0), *shapes)
    near_next = unpack(fetch(packed, 1, 0), *shapes)
    near_next, ride = lax.optimization_barrier((near_next, ride))
    near = fold(near_last, near_next)
    far = fold(far_last, far_next)
    held = jnp.where(even, pack(*near), pack(*far))
    swap = [(2 * c, 2 * c + 1) for c in range(chips)] + [(2 * c + 1, 2 * c) for c in range(chips)]
    other = shifted(held, axis, swap)
    near_gain, near_state = unpack(jnp.where(even, held, other), *shapes)
    _, far_state = unpack(jnp.where(even, other, held), *shapes)
    behind = near_gain[..., None, None] * far_state + near_state
    odd_entering = pair[0][..., None, None] * behind + pair[1]
    return jnp.where(even, behind, odd_entering), ride


def summed_over(value, axis):
    count = lax.axis_size(axis)
    spread = jnp.broadcast_to(value[None], (count,) + value.shape)
    return lax.all_to_all(spread, axis, 0, 0, tiled=False).sum(0)


def causal_conv(window, window_ids, weight, bias, rows):
    taps = weight.shape[0]
    own_ids = window_ids[taps - 1 :]
    extra = (1,) * (window.ndim - 1)
    result = jnp.broadcast_to(bias, (rows,) + bias.shape)
    for offset in range(taps):
        piece = window[offset : offset + rows].astype(jnp.float32)
        same = (window_ids[offset : offset + rows] == own_ids).reshape((rows,) + extra)
        result = result + jnp.where(same, piece * weight[offset].astype(jnp.float32), 0.0)
    return jax.nn.silu(result).astype(jnp.bfloat16)


def on_device(
    x_proj,
    bc_proj,
    z_proj,
    dt_raw,
    conv_x,
    conv_bc,
    bias_x,
    bias_bc,
    dt_bias,
    a_log,
    d_skip,
    norm_gain,
    seg_ids,
):
    tok_rows, inner_local = x_proj.shape
    heads_local = dt_raw.shape[1]
    state_size = STATE
    groups_local = bc_proj.shape[2] // state_size
    heads_group = heads_local // groups_local
    head_size = inner_local // heads_local
    block = STRETCH
    blocks = tok_rows // block
    margin = conv_x.shape[0] - 1
    bc_width = bc_proj.shape[1] * bc_proj.shape[2]
    rim = jnp.concatenate(
        [
            x_proj[tok_rows - margin :],
            bc_proj[tok_rows - margin :].reshape(margin, bc_width),
            jnp.broadcast_to(seg_ids[tok_rows - margin :, None].astype(jnp.bfloat16), (margin, 128)),
        ],
        axis=1,
    )
    rim = from_behind(rim, "seq", 1)
    rim_x = rim[:, :inner_local]
    rim_bc = rim[:, inner_local : inner_local + bc_width].reshape(margin, *bc_proj.shape[1:])
    rim_ids = rim[:, inner_local + bc_width]
    own_ids = seg_ids.astype(jnp.float32)
    window_ids = jnp.concatenate([rim_ids.astype(jnp.float32), own_ids])
    x_conv = causal_conv(jnp.concatenate([rim_x, x_proj]), window_ids, conv_x, bias_x, tok_rows)
    bc_conv = causal_conv(
        jnp.concatenate([rim_bc, bc_proj]), window_ids, conv_bc, bias_bc, tok_rows
    )
    step_size = jax.nn.softplus(dt_raw + dt_bias)
    log_decay = step_size * -jnp.exp(a_log)
    cumul = jnp.cumsum(log_decay.reshape(blocks, block, heads_local), axis=1)
    cum_heads = cumul.reshape(blocks, block, groups_local, heads_group).transpose(0, 2, 3, 1)
    step_heads = step_size.reshape(blocks, block, groups_local, heads_group).transpose(0, 2, 3, 1)
    block_ids = own_ids.reshape(blocks, block)
    before_ids = window_ids[margin - 1 : margin - 1 + tok_rows : block]
    b_in = bc_conv[:, 0].reshape(blocks, block, groups_local, state_size)
    c_out = bc_conv[:, 1].reshape(blocks, block, groups_local, state_size)
    lower = jnp.tril(jnp.ones((block, block), dtype=bool))
    same = (block_ids[:, :, None] == block_ids[:, None, :]) & lower
    scores = jnp.einsum("cqgn,csgn->cgqs", c_out, b_in, preferred_element_type=jnp.float32)
    same_heads = same[:, None, None]
    spread = cum_heads[..., :, None] - cum_heads[..., None, :]
    decay = jnp.where(same_heads, jnp.exp(jnp.where(same_heads, spread, 0.0)), 0.0)
    mixing = (scores[:, :, None] * decay * step_heads[..., None, :]).astype(jnp.bfloat16)
    x_heads = x_conv.reshape(blocks, block, groups_local, heads_group, head_size)
    y_intra = jnp.einsum("cghqs,csghp->cqghp", mixing, x_heads, preferred_element_type=jnp.float32)
    tail_same = (block_ids == block_ids[:, -1:]).astype(jnp.float32)[:, None, None, :]
    weights = jnp.exp(cum_heads[..., -1:] - cum_heads) * step_heads * tail_same
    b_weighted = (
        b_in.transpose(0, 2, 1, 3)[:, :, None].astype(jnp.float32) * weights[..., None]
    ).astype(jnp.bfloat16)
    increment = jnp.einsum(
        "cghsn,csghp->cghpn", b_weighted, x_heads, preferred_element_type=jnp.float32
    )
    carry_gain = (
        jnp.exp(cum_heads[..., -1])
        * (block_ids[:, -1] == before_ids).astype(jnp.float32)[:, None, None]
    )
    link = (
        jnp.exp(cum_heads)
        * (block_ids == before_ids[:, None]).astype(jnp.float32)[:, None, None, :]
    )
    c_float = c_out.astype(jnp.float32)

    def recur(start_state):
        stacked = []
        current = start_state
        for index in range(blocks):
            stacked.append(current)
            current = carry_gain[index][..., None, None] * current + increment[index]
        return (jnp.stack(stacked), current)

    empty = jnp.zeros((groups_local, heads_group, head_size, state_size), jnp.float32)
    zero_states, summary = recur(empty)
    device_gain = carry_gain[0] * carry_gain[1]
    skip = d_skip.reshape(groups_local, heads_group)[..., None]
    base = y_intra + skip * x_heads.astype(jnp.float32)
    gate = jax.nn.silu(z_proj.astype(jnp.float32))
    entering, (base, gate) = entering_state(device_gain, summary, "seq", (base, gate))
    states, _ = recur(entering)
    product = jnp.einsum("cqgn,cghpn->cqghp", c_float, states, precision=lax.Precision.HIGHEST)
    y_inter = product * link.transpose(0, 3, 1, 2)[..., None]
    mixed = base + y_inter
    gated = mixed.reshape(tok_rows, inner_local) * gate
    squares = summed_over(jnp.sum(gated * gated, axis=-1), "tp")
    scale = lax.rsqrt(squares / (inner_local * lax.axis_size("tp")) + 1e-05)
    return (gated * scale[:, None] * norm_gain).astype(jnp.bfloat16)


def solution(mesh):
    in_specs = (
        P("seq", "tp"),
        P("seq", None, "tp"),
        P("seq", "tp"),
        P("seq", "tp"),
        P(None, "tp"),
        P(None, None, "tp"),
        P("tp"),
        P(None, "tp"),
        P("tp"),
        P("tp"),
        P("tp"),
        P("tp"),
        P("seq"),
    )
    out_specs = P("seq", "tp")
    return jax.shard_map(
        on_device, mesh=mesh, in_specs=in_specs, out_specs=out_specs, check_vma=False
    )
```
